32 devices in a mesh: groups: 2 (over y), wide: 4 (over z), ctx: 4 (over x, core).
Axes of the slice: x: 2, y: 2, z: 4, core: 2. Of those that a mesh axis runs over, the one named last changes fastest.
Arguments:
- queries: bfloat16 [4096, 6144], P(('groups', 'ctx'), 'wide'), parts along dimension 0, may hold values from -48 to 48
- key_rows: bfloat16 [4096, 1024], P(('groups', 'ctx')), parts along dimension 0, may hold values from -48 to 48
- value_head_rows: bfloat16 [4096, 1024], P(('groups', 'ctx')), parts along dimension 0, may hold values from -18 to 18
- residual: bfloat16 [4096, 6144], P(('groups', 'ctx'), 'wide'), parts along dimension 0, may hold values from -48 to 48
- out_weight: bfloat16 [6144, 6144], P('wide'), may hold values from -0.109375 to 0.109375
- norm_gain: bfloat16 [6144], P('wide'), may hold values from 0.25 to 1.75
- router_weight: bfloat16 [6144, 8], P('wide'), may hold values from -0.078125 to 0.078125
- gate_weight: bfloat16 [6144, 8192], P('wide', 'ctx'), may hold values from -0.078125 to 0.078125
- up_weight: bfloat16 [6144, 8192], P('wide', 'ctx'), may hold values from -0.078125 to 0.078125
- down_weight: bfloat16 [8192, 6144], P('ctx', 'wide'), may hold values from -0.0625 to 0.0625
- expert_ids: int32 [4096, 2], P('groups'), parts along dimension 0, may hold values from 0 to 7, as said below
- slot_ids: int32 [4096, 2], P('groups'), parts along dimension 0, may hold values from -1 to 639, as said below
Outputs:
- layer_out: bfloat16 [4096, 6144], P(('groups', 'ctx'), 'wide'), parts along dimension 0
The draws below stay inside these ranges and needn't reach their ends.
There are 2 independent parts, one for each index of `groups`. The reference program is written for one: setup_inputs(seed, part) draws one part's arguments, and reference() takes and returns one part's arrays. A program takes and returns all parts, laid end to end along the dimension named above; an argument that names none is the same for every part. Nothing has to cross between parts.
Inputs may be any that keep to these rules, and one draw needn't show every extreme that they name: `expert_ids`: each row names 2 different experts; expert 0 is named by at least 704 rows, so its buffer is full in every draw. `slot_ids`: the rows naming one expert take its buffer rows 0, 1, 2 and so on in the order of positions (for one position, the earlier column first); once 640 rows are taken, further choices of that expert hold -1. Rows of one expert's buffer are never shared.
All inputs are finite; a program needn't handle non-finite values.
Results may differ from the reference program's by a relative error of at most 0.015.
Values may be sent and summed in bfloat16 or wider, within the bound.
No kernel may reach another device: no remote copies, remote signals or barrier semaphores. Data moves between devices by JAX's collectives and lax.ppermute only.
A program may use at most 192 MiB of HBM per device.

```python
import math
import jax
import jax.numpy as jnp
from jax import lax

D = 6144
QUERY_HEADS = 48
KEY_VALUE_HEADS = 8
HEAD_SIZE = 128
EXPERTS = 8
TOP = 2
FF = 8192
DOCUMENT_LENGTH = 2048
CAP = 640


def route_draw(key):
    route_key = jax.random.fold_in(key, 11)
    order_key, score_key, bias_key = jax.random.split(route_key, 3)
    forced_count = CAP + DOCUMENT_LENGTH // 32
    shuffled = jax.random.permutation(order_key, DOCUMENT_LENGTH)
    forced = jnp.zeros((DOCUMENT_LENGTH,), jnp.int32).at[shuffled[:forced_count]].set(1)
    scores = jax.random.randint(score_key, (DOCUMENT_LENGTH, EXPERTS), 0, 65536)
    biases = jax.random.randint(bias_key, (EXPERTS,), 0, 32768)
    columns = jnp.arange(EXPERTS, dtype=jnp.int32)
    ranked = (scores + biases[None, :]) * EXPERTS + columns[None, :]
    ranked = ranked + jnp.where(jnp.logical_and(columns[None, :] == 0, forced[:, None] == 1), 1 << 22, 0)
    chosen = lax.top_k(ranked, TOP)[1].astype(jnp.int32)
    onehot = (chosen[:, :, None] == columns[None, None, :]).astype(jnp.int32).reshape(DOCUMENT_LENGTH * TOP, EXPERTS)
    counted = jnp.cumsum(onehot, axis=0) - 1
    ranking = jnp.sum(onehot * counted, axis=1).reshape(DOCUMENT_LENGTH, TOP)
    slot_rank = jnp.where(ranking < CAP, ranking, -1).astype(jnp.int32)
    return (chosen, slot_rank)


def draw_expert_ids(key, part):
    return route_draw(key)[0]


def draw_slot_ids(key, part):
    return route_draw(key)[1]


def draw_queries(key, part):
    simple_key = jax.random.fold_in(key, 1)
    return jnp.clip(jax.random.normal(simple_key, (DOCUMENT_LENGTH, QUERY_HEADS * HEAD_SIZE), jnp.float32), -6.0, 6.0).astype(jnp.bfloat16)


def draw_key_rows(key, part):
    simple_key = jax.random.fold_in(key, 2)
    return jnp.clip(jax.random.normal(simple_key, (DOCUMENT_LENGTH, KEY_VALUE_HEADS * HEAD_SIZE), jnp.float32), -6.0, 6.0).astype(jnp.bfloat16)


def draw_residual(key, part):
    base_key, row_key, col_key = jax.random.split(jax.random.fold_in(key, 3), 3)
    entries = jnp.clip(jax.random.normal(base_key, (DOCUMENT_LENGTH, D), jnp.float32), -5.0, 5.0)
    row_scale = jnp.exp(jax.random.uniform(row_key, (DOCUMENT_LENGTH, 1), jnp.float32, -1.204, 1.0986))
    col_scale = jnp.exp(jax.random.uniform(col_key, (1, D), jnp.float32, -1.204, 1.0986))
    return (entries * row_scale * col_scale).astype(jnp.bfloat16)


def strengthened(array, key, source, target, blocks, factor):
    owner, partner = [(jnp.arange(array.shape[position]) // (array.shape[position] // blocks)).reshape([-1 if axis == position else 1 for axis in range(array.ndim)]) for position in (source, target)]
    chosen = jax.random.permutation(key, blocks)[partner]
    strong = (owner == chosen) | (owner == (partner + blocks // 2) % blocks)
    return jnp.where(strong, factor * array, array)


def levels(key, extent, pieces, smallest, largest):
    level, own = 1.0, jax.random.fold_in(key, 6)
    for axis_at, blocks in pieces:
        steps = jnp.exp(jax.random.uniform(jax.random.fold_in(own, axis_at), (blocks,), jnp.float32, smallest / len(pieces), largest / len(pieces)))
        level = level * jnp.repeat(steps, extent[axis_at] // blocks).reshape([-1 if axis == axis_at else 1 for axis in range(len(extent))])
    return level


def noise(rng, shape, deviation, reach, cuts=(), kind=jnp.bfloat16):
    values = deviation * jax.random.normal(rng, shape, jnp.float32)
    if cuts:
        values = values * levels(rng, shape, cuts, -0.22, 0.18)
    return jnp.clip(values, -reach, reach).astype(kind)


def heavy_noise(stream_key, dims, width, reach, cuts, heavy, kind=jnp.bfloat16):
    array = width * jax.random.normal(stream_key, dims, jnp.float32)
    if cuts:
        array = array * levels(stream_key, dims, cuts, -0.22, 0.18)
    return jnp.clip(strengthened(array, jax.random.fold_in(stream_key, 3), *heavy), -reach, reach).astype(kind)


def setup_inputs(seed: int = 0, part: int = 0) -> dict:
    key_list = jax.random.split(jax.random.key(seed), 13)
    own_keys = jax.random.split(jax.random.fold_in(key_list[12], part), 13)
    return {
        "queries": draw_queries(jax.random.fold_in(jax.random.fold_in(key_list[12], part), 71), part),
        "key_rows": draw_key_rows(jax.random.fold_in(jax.random.fold_in(key_list[12], part), 71), part),
        "value_head_rows": noise(own_keys[2], (DOCUMENT_LENGTH, KEY_VALUE_HEADS * HEAD_SIZE), 3.0, 18.0, ((0, 4),)),
        "residual": draw_residual(jax.random.fold_in(jax.random.fold_in(key_list[12], part), 71), part),
        "out_weight": heavy_noise(key_list[4], (QUERY_HEADS * HEAD_SIZE, D), (QUERY_HEADS * HEAD_SIZE) ** -0.5, 0.109375, ((0, 4),), (0, 1, 4, 2.0)),
        "norm_gain": jnp.clip(1.0 + 0.15 * jax.random.normal(key_list[5], (D,), jnp.float32), 0.25, 1.75).astype(jnp.bfloat16),
        "router_weight": noise(key_list[6], (D, EXPERTS), D ** -0.5, 0.078125, ((0, 4),)),
        "gate_weight": noise(key_list[7], (D, FF), D ** -0.5, 0.078125, ((0, 4), (1, 4))),
        "up_weight": noise(key_list[8], (D, FF), D ** -0.5, 0.078125, ((0, 4), (1, 4))),
        "down_weight": noise(key_list[9], (FF, D), FF ** -0.5, 0.0625, ((0, 4), (1, 4))),
        "expert_ids": draw_expert_ids(jax.random.fold_in(jax.random.fold_in(key_list[12], part), 71), part),
        "slot_ids": draw_slot_ids(jax.random.fold_in(jax.random.fold_in(key_list[12], part), 71), part),
    }


NEG_FILL = -1e+30
EPSILON = 1e-05

def token_slots(expert_ids, slot_ids, capacity):
    in_window = jnp.logical_and(expert_ids == 0, slot_ids >= 0)
    picked = lax.optimization_barrier(jnp.max(jnp.where(in_window, slot_ids, -1), axis=1))
    return jnp.where(picked >= 0, picked, capacity).astype(jnp.int32)

def other_experts(expert_ids, slot_of_token, capacity):
    partner = lax.optimization_barrier(jnp.sum(expert_ids, axis=1)).astype(jnp.int32)
    return jnp.zeros((capacity,), jnp.int32).at[slot_of_token].set(partner, mode='drop')

def expert_hidden(gate_sum, up_sum, square_sum, logit_sum, slot_other, model_width):
    inverse_rms = lax.rsqrt(square_sum / model_width + EPSILON)
    gate_value = gate_sum * inverse_rms[:, None]
    up_value = up_sum * inverse_rms[:, None]
    logit_value = logit_sum * inverse_rms[:, None]
    columns = jnp.arange(logit_value.shape[1], dtype=jnp.int32)
    partner_logit = lax.optimization_barrier(jnp.sum(jnp.where(columns[None, :] == slot_other[:, None], logit_value, 0.0), axis=1))
    mixing = jax.nn.sigmoid(logit_value[:, 0] - partner_logit)
    return (jax.nn.silu(gate_value) * up_value * mixing[:, None]).astype(jnp.bfloat16)

def reference(queries, key_rows, value_head_rows, residual, out_weight, norm_gain, router_weight, gate_weight, up_weight, down_weight, expert_ids, slot_ids):
    query_group_width = QUERY_HEADS // KEY_VALUE_HEADS
    positions = jnp.arange(DOCUMENT_LENGTH, dtype=jnp.int32)
    allowed = positions[None, :] <= positions[:, None]
    scale_factor = 1.0 / math.sqrt(HEAD_SIZE)

    def one_head(head):
        shared = head // query_group_width
        query_head = lax.dynamic_slice_in_dim(queries, head * HEAD_SIZE, HEAD_SIZE, 1)
        key_head = lax.dynamic_slice_in_dim(key_rows, shared * HEAD_SIZE, HEAD_SIZE, 1)
        value_head = lax.dynamic_slice_in_dim(value_head_rows, shared * HEAD_SIZE, HEAD_SIZE, 1)
        scores = jnp.dot(query_head, key_head.T, preferred_element_type=jnp.float32) * scale_factor
        masked = jnp.where(allowed, scores, NEG_FILL)
        row_max = lax.optimization_barrier(jnp.max(masked, axis=1, keepdims=True))
        weights = jnp.where(allowed, jnp.exp(masked - row_max), 0.0)
        total = lax.optimization_barrier(jnp.sum(weights, axis=1, keepdims=True))
        return jnp.dot(weights.astype(jnp.bfloat16), value_head, preferred_element_type=jnp.float32) / total
    attended = lax.map(one_head, jnp.arange(QUERY_HEADS, dtype=jnp.int32))
    attended = jnp.transpose(attended, (1, 0, 2)).reshape(DOCUMENT_LENGTH, QUERY_HEADS * HEAD_SIZE).astype(jnp.bfloat16)
    projected = jnp.dot(attended, out_weight, preferred_element_type=jnp.float32)
    resid = (residual.astype(jnp.float32) + projected).astype(jnp.bfloat16)
    slot_of_token = token_slots(expert_ids, slot_ids, CAP)
    slot_other = other_experts(expert_ids, slot_of_token, CAP)
    buffer = jnp.zeros((CAP, D), jnp.bfloat16).at[slot_of_token].set(resid, mode='drop')
    buffer_wide = buffer.astype(jnp.float32)
    square_sum = lax.optimization_barrier(jnp.sum(buffer_wide * buffer_wide, axis=1))
    scaled = (buffer_wide * norm_gain.astype(jnp.float32)[None, :]).astype(jnp.bfloat16)
    gate_sum = jnp.dot(scaled, gate_weight, preferred_element_type=jnp.float32)
    up_sum = jnp.dot(scaled, up_weight, preferred_element_type=jnp.float32)
    logit_sum = jnp.dot(scaled, router_weight, preferred_element_type=jnp.float32)
    hidden = expert_hidden(gate_sum, up_sum, square_sum, logit_sum, slot_other, D)
    expert_out = jnp.dot(hidden, down_weight, preferred_element_type=jnp.float32)
    padded = jnp.concatenate([expert_out, jnp.zeros((1, D), jnp.float32)], axis=0)
    routed = jnp.take(padded, slot_of_token, axis=0)
    return (resid.astype(jnp.float32) + routed).astype(jnp.bfloat16)
```

```python
import math

import jax
import jax.numpy as jnp
from jax import lax
from jax.sharding import PartitionSpec as P

D = 6144
QUERY_HEADS = 48
KEY_VALUE_HEADS = 8
HEAD_SIZE = 128


NEG_FILL = -1e30
EPSILON = 1e-05


def token_slots(expert_ids, slot_ids, capacity):
    in_window = jnp.logical_and(expert_ids == 0, slot_ids >= 0)
    picked = jnp.max(jnp.where(in_window, slot_ids, -1), axis=1)
    return jnp.where(picked >= 0, picked, capacity)


def other_experts(expert_ids, slot_of_token, capacity):
    partner = jnp.sum(expert_ids, axis=1)
    return jnp.zeros((capacity,), jnp.int32).at[slot_of_token].set(partner, mode="drop")


def expert_hidden(gate_sum, up_sum, square_sum, logit_sum, slot_other, model_width):
    inverse_rms = lax.rsqrt(square_sum / model_width + EPSILON)
    gate_value = gate_sum * inverse_rms[:, None]
    up_value = up_sum * inverse_rms[:, None]
    logit_value = logit_sum * inverse_rms[:, None]
    columns = jnp.arange(logit_value.shape[1], dtype=jnp.int32)
    partner_logit = jnp.sum(
        jnp.where(columns[None, :] == slot_other[:, None], logit_value, 0.0), axis=1
    )
    mixing = jax.nn.sigmoid(logit_value[:, 0] - partner_logit)
    return (jax.nn.silu(gate_value) * up_value * mixing[:, None]).astype(jnp.bfloat16)


def local(
    queries,
    key_rows,
    value_head_rows,
    residual,
    out_weight,
    norm_gain,
    router_weight,
    gate_weight,
    up_weight,
    down_weight,
    expert_ids,
    slot_ids,
):
    ctx_count = lax.axis_size("ctx")
    wide_index = lax.axis_index("wide")
    ctx_index = lax.axis_index("ctx")
    rows_local = queries.shape[0]
    heads_local = queries.shape[1] // HEAD_SIZE
    query_group_width = QUERY_HEADS // KEY_VALUE_HEADS
    shared_heads = max(1, heads_local // query_group_width)
    per_shared = heads_local // shared_heads
    first_shared = wide_index * heads_local // query_group_width
    key_used = lax.dynamic_slice_in_dim(
        key_rows, first_shared * HEAD_SIZE, shared_heads * HEAD_SIZE, 1
    )
    value_used = lax.dynamic_slice_in_dim(
        value_head_rows, first_shared * HEAD_SIZE, shared_heads * HEAD_SIZE, 1
    )
    query_blocks = queries.reshape(rows_local, shared_heads, per_shared, HEAD_SIZE)
    query_pos = ctx_index * rows_local + jnp.arange(rows_local, dtype=jnp.int32)
    last_query = ctx_index * rows_local + rows_local - 1
    scale_factor = 1.0 / math.sqrt(HEAD_SIZE)
    start_state = (
        jnp.full((shared_heads, per_shared, rows_local), -jnp.inf, jnp.float32),
        jnp.zeros((shared_heads, per_shared, rows_local), jnp.float32),
        jnp.zeros((shared_heads, per_shared, rows_local, HEAD_SIZE), jnp.float32),
    )
    packed_kv = lax.all_gather(
        jnp.concatenate([key_used, value_used], axis=1), "ctx", axis=0, tiled=True
    )
    pieces = (
        packed_kv[:, : shared_heads * HEAD_SIZE],
        packed_kv[:, shared_heads * HEAD_SIZE :],
    )

    def update(state):
        running_max, running_sum, running_acc = state
        key_piece = pieces[0].reshape(-1, shared_heads, HEAD_SIZE)
        value_piece = pieces[1].reshape(-1, shared_heads, HEAD_SIZE)
        scores = (
            jnp.einsum(
                "skqd,rkd->kqsr", query_blocks, key_piece, preferred_element_type=jnp.float32
            )
            * scale_factor
        )
        key_pos = jnp.arange(key_piece.shape[0], dtype=jnp.int32)
        allowed = (key_pos[None, :] <= query_pos[:, None])[None, None, :, :]
        masked = jnp.where(allowed, scores, NEG_FILL)
        new_max = jnp.max(masked, axis=-1)
        weights = jnp.where(allowed, jnp.exp(masked - new_max[..., None]), 0.0)
        decay = jnp.exp(running_max - new_max)
        new_sum = running_sum * decay + jnp.sum(weights, axis=-1)
        added = jnp.einsum(
            "kqsr,rkd->kqsd",
            weights.astype(jnp.bfloat16),
            value_piece,
            preferred_element_type=jnp.float32,
        )
        return (new_max, new_sum, running_acc * decay[..., None] + added)

    final_max, final_sum, final_acc = lax.cond(
        jnp.int32(0) > last_query, lambda state: state, update, start_state
    )
    attended = final_acc / final_sum[..., None]
    attended = (
        jnp.transpose(attended, (2, 0, 1, 3))
        .reshape(rows_local, heads_local * HEAD_SIZE)
        .astype(jnp.bfloat16)
    )
    partial_out = jnp.dot(attended, out_weight, preferred_element_type=jnp.float32)
    head_sum = lax.psum_scatter(
        partial_out.astype(jnp.bfloat16), "wide", scatter_dimension=1, tiled=True
    ).astype(jnp.float32)
    resid = (residual.astype(jnp.float32) + head_sum).astype(jnp.bfloat16)
    seq_len = rows_local * ctx_count
    capacity = seq_len * 5 // 16
    width_local = resid.shape[1]
    wide_count = lax.axis_size("wide")
    chunk = capacity // wide_count
    slot_of_token = token_slots(expert_ids, slot_ids, capacity)
    slot_other = other_experts(expert_ids, slot_of_token, capacity)
    slot_local = lax.dynamic_slice_in_dim(slot_of_token, ctx_index * rows_local, rows_local)
    own_rows = jnp.zeros((capacity, width_local), jnp.bfloat16).at[slot_local].set(
        resid, mode="drop"
    )
    buffer = lax.psum(own_rows, "ctx")
    buffer_wide = buffer.astype(jnp.float32)
    square_part = jnp.sum(buffer_wide * buffer_wide, axis=1)
    scaled = (buffer_wide * norm_gain.astype(jnp.float32)[None, :]).astype(jnp.bfloat16)
    gate_part = jnp.dot(scaled, gate_weight, preferred_element_type=jnp.float32)
    up_part = jnp.dot(scaled, up_weight, preferred_element_type=jnp.float32)
    logit_part = jnp.dot(scaled, router_weight, preferred_element_type=jnp.float32)
    hidden_local = gate_part.shape[1]
    experts = logit_part.shape[1]
    pad = 128 - (experts + 1) % 128
    packed = jnp.concatenate(
        [
            gate_part,
            up_part,
            logit_part,
            square_part[:, None],
            jnp.zeros((capacity, pad), jnp.float32),
        ],
        axis=1,
    ).astype(jnp.bfloat16)
    reduced = lax.psum_scatter(packed, "wide", scatter_dimension=0, tiled=True).astype(
        jnp.float32
    )
    gate_sum = reduced[:, :hidden_local]
    up_sum = reduced[:, hidden_local : 2 * hidden_local]
    logit_sum = reduced[:, 2 * hidden_local : 2 * hidden_local + experts]
    square_sum = reduced[:, 2 * hidden_local + experts]
    other_chunk = lax.dynamic_slice_in_dim(slot_other, wide_index * chunk, chunk)
    hidden_chunk = expert_hidden(gate_sum, up_sum, square_sum, logit_sum, other_chunk, D)
    hidden = lax.all_gather(hidden_chunk, "wide", axis=0, tiled=True)
    expert_part = jnp.dot(hidden, down_weight, preferred_element_type=jnp.float32)
    expert_sum = lax.psum(expert_part.astype(jnp.bfloat16), "ctx")
    expert_pad = jnp.concatenate(
        [expert_sum, jnp.zeros((1, width_local), jnp.bfloat16)], axis=0
    )
    moe_rows = jnp.take(expert_pad, slot_local, axis=0).astype(jnp.float32)
    return (resid.astype(jnp.float32) + moe_rows).astype(jnp.bfloat16)


def solution(mesh):
    placed = (
        P(("groups", "ctx"), "wide"),
        P(("groups", "ctx"), None),
        P(("groups", "ctx"), None),
        P(("groups", "ctx"), "wide"),
        P("wide", None),
        P("wide"),
        P("wide", None),
        P("wide", "ctx"),
        P("wide", "ctx"),
        P("ctx", "wide"),
        P("groups", None),
        P("groups", None),
    )
    return jax.shard_map(
        local, mesh=mesh, in_specs=placed, out_specs=P(("groups", "ctx"), "wide"), check_vma=False
    )
```

```python
import functools
import math

import jax
import jax.numpy as jnp
from jax import lax
from jax.experimental import pallas as pl
from jax.experimental.pallas import tpu as pltpu
from jax.sharding import PartitionSpec as P

D = 6144
QUERY_HEADS = 48
KEY_VALUE_HEADS = 8
HEAD_SIZE = 128


NEG_FILL = -1e30
EPSILON = 1e-05


def token_slots(expert_ids, slot_ids, capacity):
    in_window = jnp.logical_and(expert_ids == 0, slot_ids >= 0)
    picked = jnp.max(jnp.where(in_window, slot_ids, -1), axis=1)
    return jnp.where(picked >= 0, picked, capacity)


def other_experts(expert_ids, slot_of_token, capacity):
    partner = jnp.sum(expert_ids, axis=1)
    return jnp.zeros((capacity,), jnp.int32).at[slot_of_token].set(partner, mode="drop")


def expert_hidden(gate_sum, up_sum, square_sum, logit_sum, slot_other, model_width):
    inverse_rms = lax.rsqrt(square_sum / model_width + EPSILON)
    gate_value = gate_sum * inverse_rms[:, None]
    up_value = up_sum * inverse_rms[:, None]
    logit_value = logit_sum * inverse_rms[:, None]
    columns = jnp.arange(logit_value.shape[1], dtype=jnp.int32)
    partner_logit = jnp.sum(
        jnp.where(columns[None, :] == slot_other[:, None], logit_value, 0.0), axis=1
    )
    mixing = jax.nn.sigmoid(logit_value[:, 0] - partner_logit)
    return (jax.nn.silu(gate_value) * up_value * mixing[:, None]).astype(jnp.bfloat16)


def attention_kernel(offset_ref, q_ref, k_ref, v_ref, o_ref, *, per_shared, block_q, scale):
    seq = k_ref.shape[0]
    first = offset_ref[0] + pl.program_id(1) * block_q
    rows = first + lax.broadcasted_iota(jnp.int32, (block_q, seq), 0)
    cols = lax.broadcasted_iota(jnp.int32, (block_q, seq), 1)
    allowed = cols <= rows
    keys = k_ref[...]
    values = v_ref[...]
    for head in range(per_shared):
        query = q_ref[:, head * HEAD_SIZE : (head + 1) * HEAD_SIZE]
        scores = (
            lax.dot_general(
                query, keys, (((1,), (1,)), ((), ())), preferred_element_type=jnp.float32
            )
            * scale
        )
        masked = jnp.where(allowed, scores, NEG_FILL)
        row_max = jnp.max(masked, axis=1, keepdims=True)
        weights = jnp.exp(masked - row_max)
        total = jnp.sum(weights, axis=1, keepdims=True)
        acc = jnp.dot(weights.astype(jnp.bfloat16), values, preferred_element_type=jnp.float32)
        o_ref[:, head * HEAD_SIZE : (head + 1) * HEAD_SIZE] = (acc / total).astype(o_ref.dtype)


def attend(queries, packed_kv, offset, shared_heads, per_shared, interpret=False):
    rows_local = queries.shape[0]
    seq = packed_kv.shape[0]
    block_q = 256 if seq <= 2048 else 128
    block_q = min(block_q, rows_local)
    width = per_shared * HEAD_SIZE
    kernel = functools.partial(
        attention_kernel,
        per_shared=per_shared,
        block_q=block_q,
        scale=1.0 / math.sqrt(HEAD_SIZE),
    )
    grid_spec = pltpu.PrefetchScalarGridSpec(
        num_scalar_prefetch=1,
        grid=(shared_heads, rows_local // block_q),
        in_specs=[
            pl.BlockSpec((block_q, width), lambda g, b, off: (b, g)),
            pl.BlockSpec((seq, HEAD_SIZE), lambda g, b, off: (0, g)),
            pl.BlockSpec((seq, HEAD_SIZE), lambda g, b, off: (0, shared_heads + g)),
        ],
        out_specs=pl.BlockSpec((block_q, width), lambda g, b, off: (b, g)),
    )
    return pl.pallas_call(
        kernel,
        grid_spec=grid_spec,
        out_shape=jax.ShapeDtypeStruct((rows_local, shared_heads * width), jnp.bfloat16),
        compiler_params=pltpu.CompilerParams(vmem_limit_bytes=48 * 1024 * 1024),
        interpret=interpret,
    )(offset, queries, packed_kv, packed_kv)


def local(
    queries,
    key_rows,
    value_head_rows,
    residual,
    out_weight,
    norm_gain,
    router_weight,
    gate_weight,
    up_weight,
    down_weight,
    expert_ids,
    slot_ids,
):
    ctx_count = lax.axis_size("ctx")
    wide_index = lax.axis_index("wide")
    ctx_index = lax.axis_index("ctx")
    rows_local = queries.shape[0]
    heads_local = queries.shape[1] // HEAD_SIZE
    query_group_width = QUERY_HEADS // KEY_VALUE_HEADS
    shared_heads = max(1, heads_local // query_group_width)
    per_shared = heads_local // shared_heads
    first_shared = wide_index * heads_local // query_group_width
    key_used = lax.dynamic_slice_in_dim(
        key_rows, first_shared * HEAD_SIZE, shared_heads * HEAD_SIZE, 1
    )
    value_used = lax.dynamic_slice_in_dim(
        value_head_rows, first_shared * HEAD_SIZE, shared_heads * HEAD_SIZE, 1
    )
    packed_kv = lax.all_gather(
        jnp.concatenate([key_used, value_used], axis=1), "ctx", axis=0, tiled=True
    )
    offset = jnp.reshape(ctx_index * rows_local, (1,)).astype(jnp.int32)
    attended = attend(queries, packed_kv, offset, shared_heads, per_shared)
    partial_out = jnp.dot(attended, out_weight, preferred_element_type=jnp.float32)
    head_sum = lax.psum_scatter(
        partial_out.astype(jnp.bfloat16), "wide", scatter_dimension=1, tiled=True
    ).astype(jnp.float32)
    resid = (residual.astype(jnp.float32) + head_sum).astype(jnp.bfloat16)
    seq_len = rows_local * ctx_count
    capacity = seq_len * 5 // 16
    width_local = resid.shape[1]
    wide_count = lax.axis_size("wide")
    chunk = capacity // wide_count
    slot_of_token = token_slots(expert_ids, slot_ids, capacity)
    slot_other = other_experts(expert_ids, slot_of_token, capacity)
    slot_local = lax.dynamic_slice_in_dim(slot_of_token, ctx_index * rows_local, rows_local)
    own_rows = jnp.zeros((capacity, width_local), jnp.bfloat16).at[slot_local].set(
        resid, mode="drop"
    )
    buffer = lax.psum(own_rows, "ctx")
    buffer_wide = buffer.astype(jnp.float32)
    square_part = jnp.sum(buffer_wide * buffer_wide, axis=1)
    scaled = (buffer_wide * norm_gain.astype(jnp.float32)[None, :]).astype(jnp.bfloat16)
    gate_part = jnp.dot(scaled, gate_weight, preferred_element_type=jnp.float32)
    up_part = jnp.dot(scaled, up_weight, preferred_element_type=jnp.float32)
    logit_part = jnp.dot(scaled, router_weight, preferred_element_type=jnp.float32)
    hidden_local = gate_part.shape[1]
    experts = logit_part.shape[1]
    pad = 128 - (experts + 1) % 128
    packed = jnp.concatenate(
        [
            gate_part,
            up_part,
            logit_part,
            square_part[:, None],
            jnp.zeros((capacity, pad), jnp.float32),
        ],
        axis=1,
    ).astype(jnp.bfloat16)
    reduced = lax.psum_scatter(packed, "wide", scatter_dimension=0, tiled=True).astype(
        jnp.float32
    )
    gate_sum = reduced[:, :hidden_local]
    up_sum = reduced[:, hidden_local : 2 * hidden_local]
    logit_sum = reduced[:, 2 * hidden_local : 2 * hidden_local + experts]
    square_sum = reduced[:, 2 * hidden_local + experts]
    other_chunk = lax.dynamic_slice_in_dim(slot_other, wide_index * chunk, chunk)
    hidden_chunk = expert_hidden(gate_sum, up_sum, square_sum, logit_sum, other_chunk, D)
    hidden = lax.all_gather(hidden_chunk, "wide", axis=0, tiled=True)
    expert_part = jnp.dot(hidden, down_weight, preferred_element_type=jnp.float32)
    expert_sum = lax.psum(expert_part.astype(jnp.bfloat16), "ctx")
    expert_pad = jnp.concatenate(
        [expert_sum, jnp.zeros((1, width_local), jnp.bfloat16)], axis=0
    )
    moe_rows = jnp.take(expert_pad, slot_local, axis=0).astype(jnp.float32)
    return (resid.astype(jnp.float32) + moe_rows).astype(jnp.bfloat16)


def solution(mesh):
    placed = (
        P(("groups", "ctx"), "wide"),
        P(("groups", "ctx"), None),
        P(("groups", "ctx"), None),
        P(("groups", "ctx"), "wide"),
        P("wide", None),
        P("wide"),
        P("wide", None),
        P("wide", "ctx"),
        P("wide", "ctx"),
        P("ctx", "wide"),
        P("groups", None),
        P("groups", None),
    )
    return jax.shard_map(
        local, mesh=mesh, in_specs=placed, out_specs=P(("groups", "ctx"), "wide"), check_vma=False
    )
```

```python
import functools
import math

import jax
import jax.numpy as jnp
from jax import lax
from jax.experimental import pallas as pl
from jax.experimental.pallas import tpu as pltpu
from jax.sharding import PartitionSpec as P

D = 6144
QUERY_HEADS = 48
KEY_VALUE_HEADS = 8
HEAD_SIZE = 128


NEG_FILL = -1e30
EPSILON = 1e-05


def token_slots(expert_ids, slot_ids, capacity):
    in_window = jnp.logical_and(expert_ids == 0, slot_ids >= 0)
    picked = jnp.max(jnp.where(in_window, slot_ids, -1), axis=1)
    return jnp.where(picked >= 0, picked, capacity)


def other_experts(expert_ids, slot_of_token, capacity):
    partner = jnp.sum(expert_ids, axis=1)
    return jnp.zeros((capacity,), jnp.int32).at[slot_of_token].set(partner, mode="drop")


def expert_hidden(gate_sum, up_sum, square_sum, logit_sum, slot_other, model_width):
    inverse_rms = lax.rsqrt(square_sum / model_width + EPSILON)
    gate_value = gate_sum * inverse_rms[:, None]
    up_value = up_sum * inverse_rms[:, None]
    logit_value = logit_sum * inverse_rms[:, None]
    columns = jnp.arange(logit_value.shape[1], dtype=jnp.int32)
    partner_logit = jnp.sum(
        jnp.where(columns[None, :] == slot_other[:, None], logit_value, 0.0), axis=1
    )
    mixing = jax.nn.sigmoid(logit_value[:, 0] - partner_logit)
    return (jax.nn.silu(gate_value) * up_value * mixing[:, None]).astype(jnp.bfloat16)


def attention_kernel(offset_ref, q_ref, k_ref, v_ref, o_ref, *, per_shared, block_q, scale):
    seq = k_ref.shape[0]
    first = offset_ref[0] + pl.program_id(1) * block_q
    rows = first + lax.broadcasted_iota(jnp.int32, (block_q, seq), 0)
    cols = lax.broadcasted_iota(jnp.int32, (block_q, seq), 1)
    allowed = cols <= rows
    keys = k_ref[...]
    values = v_ref[...]
    for head in range(per_shared):
        query = q_ref[:, head * HEAD_SIZE : (head + 1) * HEAD_SIZE]
        scores = (
            lax.dot_general(
                query, keys, (((1,), (1,)), ((), ())), preferred_element_type=jnp.float32
            )
            * scale
        )
        masked = jnp.where(allowed, scores, NEG_FILL)
        row_max = jnp.max(masked, axis=1, keepdims=True)
        weights = jnp.exp(masked - row_max)
        total = jnp.sum(weights, axis=1, keepdims=True)
        acc = jnp.dot(weights.astype(jnp.bfloat16), values, preferred_element_type=jnp.float32)
        o_ref[:, head * HEAD_SIZE : (head + 1) * HEAD_SIZE] = (acc / total).astype(o_ref.dtype)


def attend(queries, packed_kv, offset, shared_heads, per_shared, interpret=False):
    rows_local = queries.shape[0]
    seq = packed_kv.shape[0]
    block_q = 256 if seq <= 2048 else 128
    block_q = min(block_q, rows_local)
    width = per_shared * HEAD_SIZE
    kernel = functools.partial(
        attention_kernel,
        per_shared=per_shared,
        block_q=block_q,
        scale=1.0 / math.sqrt(HEAD_SIZE),
    )
    grid_spec = pltpu.PrefetchScalarGridSpec(
        num_scalar_prefetch=1,
        grid=(shared_heads, rows_local // block_q),
        in_specs=[
            pl.BlockSpec((block_q, width), lambda g, b, off: (b, g)),
            pl.BlockSpec((seq, HEAD_SIZE), lambda g, b, off: (0, g)),
            pl.BlockSpec((seq, HEAD_SIZE), lambda g, b, off: (0, shared_heads + g)),
        ],
        out_specs=pl.BlockSpec((block_q, width), lambda g, b, off: (b, g)),
    )
    return pl.pallas_call(
        kernel,
        grid_spec=grid_spec,
        out_shape=jax.ShapeDtypeStruct((rows_local, shared_heads * width), jnp.bfloat16),
        compiler_params=pltpu.CompilerParams(vmem_limit_bytes=48 * 1024 * 1024),
        interpret=interpret,
    )(offset, queries, packed_kv, packed_kv)


def local(
    queries,
    key_rows,
    value_head_rows,
    residual,
    out_weight,
    norm_gain,
    router_weight,
    gate_weight,
    up_weight,
    down_weight,
    expert_ids,
    slot_ids,
):
    ctx_count = lax.axis_size("ctx")
    wide_index = lax.axis_index("wide")
    ctx_index = lax.axis_index("ctx")
    rows_local = queries.shape[0]
    heads_local = queries.shape[1] // HEAD_SIZE
    query_group_width = QUERY_HEADS // KEY_VALUE_HEADS
    shared_heads = max(1, heads_local // query_group_width)
    per_shared = heads_local // shared_heads
    first_shared = wide_index * heads_local // query_group_width
    key_used = lax.dynamic_slice_in_dim(
        key_rows, first_shared * HEAD_SIZE, shared_heads * HEAD_SIZE, 1
    )
    value_used = lax.dynamic_slice_in_dim(
        value_head_rows, first_shared * HEAD_SIZE, shared_heads * HEAD_SIZE, 1
    )
    packed_kv = lax.all_gather(
        jnp.concatenate([key_used, value_used], axis=1), "ctx", axis=0, tiled=True
    )
    offset = jnp.reshape(ctx_index * rows_local, (1,)).astype(jnp.int32)
    attended = attend(queries, packed_kv, offset, shared_heads, per_shared)
    partial_out = jnp.dot(attended, out_weight, preferred_element_type=jnp.float32)
    head_sum = lax.psum_scatter(
        partial_out.astype(jnp.bfloat16), "wide", scatter_dimension=1, tiled=True
    ).astype(jnp.float32)
    resid = (residual.astype(jnp.float32) + head_sum).astype(jnp.bfloat16)
    seq_len = rows_local * ctx_count
    capacity = seq_len * 5 // 16
    width_local = resid.shape[1]
    wide_count = lax.axis_size("wide")
    chunk = capacity // wide_count
    slot_of_token = token_slots(expert_ids, slot_ids, capacity)
    partner = jnp.sum(expert_ids, axis=1)
    slot_local = lax.dynamic_slice_in_dim(slot_of_token, ctx_index * rows_local, rows_local)
    slot_ids_all = jnp.arange(capacity, dtype=jnp.int32)
    place = (slot_ids_all[:, None] == slot_local[None, :]).astype(jnp.bfloat16)
    own_rows = jnp.dot(place, resid, preferred_element_type=jnp.float32).astype(jnp.bfloat16)
    buffer = lax.psum(own_rows, "ctx")
    buffer_wide = buffer.astype(jnp.float32)
    square_part = jnp.sum(buffer_wide * buffer_wide, axis=1)
    scaled = (buffer_wide * norm_gain.astype(jnp.float32)[None, :]).astype(jnp.bfloat16)
    gate_part = jnp.dot(scaled, gate_weight, preferred_element_type=jnp.float32)
    up_part = jnp.dot(scaled, up_weight, preferred_element_type=jnp.float32)
    logit_part = jnp.dot(scaled, router_weight, preferred_element_type=jnp.float32)
    experts = logit_part.shape[1]
    pad = 128 - (experts + 1) % 128
    small = jnp.concatenate(
        [logit_part, square_part[:, None], jnp.zeros((capacity, pad), jnp.float32)], axis=1
    )
    gate_sum, up_sum, small_sum = (
        lax.psum_scatter(part.astype(jnp.bfloat16), "wide", scatter_dimension=0, tiled=True)
        .astype(jnp.float32)
        for part in (gate_part, up_part, small)
    )
    logit_sum = small_sum[:, :experts]
    square_sum = small_sum[:, experts]
    chunk_slots = wide_index * chunk + jnp.arange(chunk, dtype=jnp.int32)
    other_chunk = jnp.sum(
        jnp.where(chunk_slots[:, None] == slot_of_token[None, :], partner[None, :], 0), axis=1
    )
    hidden_chunk = expert_hidden(gate_sum, up_sum, square_sum, logit_sum, other_chunk, D)
    hidden = lax.all_gather(hidden_chunk, "wide", axis=0, tiled=True)
    expert_part = jnp.dot(hidden, down_weight, preferred_element_type=jnp.float32)
    expert_sum = lax.psum(expert_part.astype(jnp.bfloat16), "ctx")
    pick = (slot_local[:, None] == slot_ids_all[None, :]).astype(jnp.bfloat16)
    moe_rows = jnp.dot(pick, expert_sum, preferred_element_type=jnp.float32)
    return (resid.astype(jnp.float32) + moe_rows).astype(jnp.bfloat16)


def solution(mesh):
    placed = (
        P(("groups", "ctx"), "wide"),
        P(("groups", "ctx"), None),
        P(("groups", "ctx"), None),
        P(("groups", "ctx"), "wide"),
        P("wide", None),
        P("wide"),
        P("wide", None),
        P("wide", "ctx"),
        P("wide", "ctx"),
        P("ctx", "wide"),
        P("groups", None),
        P("groups", None),
    )
    return jax.shard_map(
        local, mesh=mesh, in_specs=placed, out_specs=P(("groups", "ctx"), "wide"), check_vma=False
    )
```

```python
import functools
import math

import jax
import jax.numpy as jnp
from jax import lax
from jax.experimental import pallas as pl
from jax.experimental.pallas import tpu as pltpu
from jax.sharding import PartitionSpec as P

D = 6144
QUERY_HEADS = 48
KEY_VALUE_HEADS = 8
HEAD_SIZE = 128


NEG_FILL = -1e30
EPSILON = 1e-05


def token_slots(expert_ids, slot_ids, capacity):
    in_window = jnp.logical_and(expert_ids == 0, slot_ids >= 0)
    picked = jnp.max(jnp.where(in_window, slot_ids, -1), axis=1)
    return jnp.where(picked >= 0, picked, capacity)


def other_experts(expert_ids, slot_of_token, capacity):
    partner = jnp.sum(expert_ids, axis=1)
    return jnp.zeros((capacity,), jnp.int32).at[slot_of_token].set(partner, mode="drop")


def expert_hidden(gate_sum, up_sum, square_sum, logit_sum, slot_other, model_width):
    inverse_rms = lax.rsqrt(square_sum / model_width + EPSILON)
    gate_value = gate_sum * inverse_rms[:, None]
    up_value = up_sum * inverse_rms[:, None]
    logit_value = logit_sum * inverse_rms[:, None]
    columns = jnp.arange(logit_value.shape[1], dtype=jnp.int32)
    partner_logit = jnp.sum(
        jnp.where(columns[None, :] == slot_other[:, None], logit_value, 0.0), axis=1
    )
    mixing = jax.nn.sigmoid(logit_value[:, 0] - partner_logit)
    return (jax.nn.silu(gate_value) * up_value * mixing[:, None]).astype(jnp.bfloat16)


def attention_kernel(offset_ref, q_ref, k_ref, v_ref, o_ref, *, per_shared, block_q, scale):
    seq = k_ref.shape[0]
    first = offset_ref[0] + pl.program_id(1) * block_q
    rows = first + lax.broadcasted_iota(jnp.int32, (block_q, seq), 0)
    cols = lax.broadcasted_iota(jnp.int32, (block_q, seq), 1)
    allowed = cols <= rows
    keys = k_ref[...]
    values = v_ref[...]
    for head in range(per_shared):
        query = q_ref[:, head * HEAD_SIZE : (head + 1) * HEAD_SIZE]
        scores = (
            lax.dot_general(
                query, keys, (((1,), (1,)), ((), ())), preferred_element_type=jnp.float32
            )
            * scale
        )
        masked = jnp.where(allowed, scores, NEG_FILL)
        row_max = jnp.max(masked, axis=1, keepdims=True)
        weights = jnp.exp(masked - row_max)
        total = jnp.sum(weights, axis=1, keepdims=True)
        acc = jnp.dot(weights.astype(jnp.bfloat16), values, preferred_element_type=jnp.float32)
        o_ref[:, head * HEAD_SIZE : (head + 1) * HEAD_SIZE] = (acc / total).astype(o_ref.dtype)


def attend(queries, packed_kv, offset, shared_heads, per_shared, interpret=False):
    rows_local = queries.shape[0]
    seq = packed_kv.shape[0]
    block_q = 256 if seq <= 2048 else 128
    block_q = min(block_q, rows_local)
    width = per_shared * HEAD_SIZE
    kernel = functools.partial(
        attention_kernel,
        per_shared=per_shared,
        block_q=block_q,
        scale=1.0 / math.sqrt(HEAD_SIZE),
    )
    grid_spec = pltpu.PrefetchScalarGridSpec(
        num_scalar_prefetch=1,
        grid=(shared_heads, rows_local // block_q),
        in_specs=[
            pl.BlockSpec((block_q, width), lambda g, b, off: (b, g)),
            pl.BlockSpec((seq, HEAD_SIZE), lambda g, b, off: (0, g)),
            pl.BlockSpec((seq, HEAD_SIZE), lambda g, b, off: (0, shared_heads + g)),
        ],
        out_specs=pl.BlockSpec((block_q, width), lambda g, b, off: (b, g)),
    )
    return pl.pallas_call(
        kernel,
        grid_spec=grid_spec,
        out_shape=jax.ShapeDtypeStruct((rows_local, shared_heads * width), jnp.bfloat16),
        compiler_params=pltpu.CompilerParams(vmem_limit_bytes=48 * 1024 * 1024),
        interpret=interpret,
    )(offset, queries, packed_kv, packed_kv)


def pair_exchange(x, axis, count, bit):
    return lax.ppermute(x, axis, perm=[(i, i ^ bit) for i in range(count)])


def gather_rows(x, axis):
    count = lax.axis_size(axis)
    if count & (count - 1):
        return lax.all_gather(x, axis, axis=0, tiled=True)
    index = lax.axis_index(axis)
    out = x
    bit = 1
    while bit < count:
        other = pair_exchange(out, axis, count, bit)
        upper = (index // bit) % 2
        size = out.shape[0]
        both = jnp.zeros((2 * size,) + out.shape[1:], out.dtype)
        both = lax.dynamic_update_slice_in_dim(both, out, upper * size, 0)
        out = lax.dynamic_update_slice_in_dim(both, other, (1 - upper) * size, 0)
        bit *= 2
    return out


def sum_rows(x, axis):
    count = lax.axis_size(axis)
    if count & (count - 1) or x.shape[0] % count:
        return lax.psum(x.astype(jnp.bfloat16), axis)
    index = lax.axis_index(axis)
    acc = x.astype(jnp.float32)
    bit = 1
    while bit < count:
        half = acc.shape[0] // 2
        upper = (index // bit) % 2
        keep = lax.dynamic_slice_in_dim(acc, upper * half, half, 0)
        send = lax.dynamic_slice_in_dim(acc, (1 - upper) * half, half, 0)
        other = pair_exchange(send.astype(jnp.bfloat16), axis, count, bit)
        acc = keep + other.astype(jnp.float32)
        bit *= 2
    out = acc.astype(jnp.bfloat16)
    bit = count // 2
    while bit >= 1:
        other = pair_exchange(out, axis, count, bit)
        upper = (index // bit) % 2
        size = out.shape[0]
        both = jnp.zeros((2 * size,) + out.shape[1:], out.dtype)
        both = lax.dynamic_update_slice_in_dim(both, out, upper * size, 0)
        out = lax.dynamic_update_slice_in_dim(both, other, (1 - upper) * size, 0)
        bit //= 2
    return out


def local(
    queries,
    key_rows,
    value_head_rows,
    residual,
    out_weight,
    norm_gain,
    router_weight,
    gate_weight,
    up_weight,
    down_weight,
    expert_ids,
    slot_ids,
):
    ctx_count = lax.axis_size("ctx")
    wide_index = lax.axis_index("wide")
    ctx_index = lax.axis_index("ctx")
    rows_local = queries.shape[0]
    heads_local = queries.shape[1] // HEAD_SIZE
    query_group_width = QUERY_HEADS // KEY_VALUE_HEADS
    shared_heads = max(1, heads_local // query_group_width)
    per_shared = heads_local // shared_heads
    first_shared = wide_index * heads_local // query_group_width
    key_used = lax.dynamic_slice_in_dim(
        key_rows, first_shared * HEAD_SIZE, shared_heads * HEAD_SIZE, 1
    )
    value_used = lax.dynamic_slice_in_dim(
        value_head_rows, first_shared * HEAD_SIZE, shared_heads * HEAD_SIZE, 1
    )
    packed_kv = gather_rows(jnp.concatenate([key_used, value_used], axis=1), "ctx")
    offset = jnp.reshape(ctx_index * rows_local, (1,)).astype(jnp.int32)
    attended = attend(queries, packed_kv, offset, shared_heads, per_shared)
    partial_out = jnp.dot(attended, out_weight, preferred_element_type=jnp.float32)
    head_sum = lax.psum_scatter(
        partial_out.astype(jnp.bfloat16), "wide", scatter_dimension=1, tiled=True
    ).astype(jnp.float32)
    resid = (residual.astype(jnp.float32) + head_sum).astype(jnp.bfloat16)
    seq_len = rows_local * ctx_count
    capacity = seq_len * 5 // 16
    width_local = resid.shape[1]
    wide_count = lax.axis_size("wide")
    chunk = capacity // wide_count
    slot_of_token = token_slots(expert_ids, slot_ids, capacity)
    partner = jnp.sum(expert_ids, axis=1)
    slot_local = lax.dynamic_slice_in_dim(slot_of_token, ctx_index * rows_local, rows_local)
    slot_ids_all = jnp.arange(capacity, dtype=jnp.int32)
    place = (slot_ids_all[:, None] == slot_local[None, :]).astype(jnp.bfloat16)
    own_rows = jnp.dot(place, resid, preferred_element_type=jnp.float32)
    buffer = sum_rows(own_rows, "ctx")
    buffer_wide = buffer.astype(jnp.float32)
    square_part = jnp.sum(buffer_wide * buffer_wide, axis=1)
    scaled = (buffer_wide * norm_gain.astype(jnp.float32)[None, :]).astype(jnp.bfloat16)
    gate_part = jnp.dot(scaled, gate_weight, preferred_element_type=jnp.float32)
    up_part = jnp.dot(scaled, up_weight, preferred_element_type=jnp.float32)
    logit_part = jnp.dot(scaled, router_weight, preferred_element_type=jnp.float32)
    experts = logit_part.shape[1]
    pad = 128 - (experts + 1) % 128
    small = jnp.concatenate(
        [logit_part, square_part[:, None], jnp.zeros((capacity, pad), jnp.float32)], axis=1
    )
    gate_sum, up_sum, small_sum = (
        lax.psum_scatter(part.astype(jnp.bfloat16), "wide", scatter_dimension=0, tiled=True)
        .astype(jnp.float32)
        for part in (gate_part, up_part, small)
    )
    logit_sum = small_sum[:, :experts]
    square_sum = small_sum[:, experts]
    chunk_slots = wide_index * chunk + jnp.arange(chunk, dtype=jnp.int32)
    other_chunk = jnp.sum(
        jnp.where(chunk_slots[:, None] == slot_of_token[None, :], partner[None, :], 0), axis=1
    )
    hidden_chunk = expert_hidden(gate_sum, up_sum, square_sum, logit_sum, other_chunk, D)
    hidden = lax.all_gather(hidden_chunk, "wide", axis=0, tiled=True)
    expert_part = jnp.dot(hidden, down_weight, preferred_element_type=jnp.float32)
    expert_sum = sum_rows(expert_part, "ctx")
    pick = (slot_local[:, None] == slot_ids_all[None, :]).astype(jnp.bfloat16)
    moe_rows = jnp.dot(pick, expert_sum, preferred_element_type=jnp.float32)
    return (resid.astype(jnp.float32) + moe_rows).astype(jnp.bfloat16)


def solution(mesh):
    placed = (
        P(("groups", "ctx"), "wide"),
        P(("groups", "ctx"), None),
        P(("groups", "ctx"), None),
        P(("groups", "ctx"), "wide"),
        P("wide", None),
        P("wide"),
        P("wide", None),
        P("wide", "ctx"),
        P("wide", "ctx"),
        P("ctx", "wide"),
        P("groups", None),
        P("groups", None),
    )
    return jax.shard_map(
        local, mesh=mesh, in_specs=placed, out_specs=P(("groups", "ctx"), "wide"), check_vma=False
    )
```

```python
import functools
import math

import jax
import jax.numpy as jnp
from jax import lax
from jax.experimental import pallas as pl
from jax.experimental.pallas import tpu as pltpu
from jax.sharding import PartitionSpec as P

D = 6144
QUERY_HEADS = 48
KEY_VALUE_HEADS = 8
HEAD_SIZE = 128


NEG_FILL = -1e30
EPSILON = 1e-05


def token_slots(expert_ids, slot_ids, capacity):
    in_window = jnp.logical_and(expert_ids == 0, slot_ids >= 0)
    picked = jnp.max(jnp.where(in_window, slot_ids, -1), axis=1)
    return jnp.where(picked >= 0, picked, capacity)


def other_experts(expert_ids, slot_of_token, capacity):
    partner = jnp.sum(expert_ids, axis=1)
    return jnp.zeros((capacity,), jnp.int32).at[slot_of_token].set(partner, mode="drop")


def expert_hidden(gate_sum, up_sum, square_sum, logit_sum, slot_other, model_width):
    inverse_rms = lax.rsqrt(square_sum / model_width + EPSILON)
    gate_value = gate_sum * inverse_rms[:, None]
    up_value = up_sum * inverse_rms[:, None]
    logit_value = logit_sum * inverse_rms[:, None]
    columns = jnp.arange(logit_value.shape[1], dtype=jnp.int32)
    partner_logit = jnp.sum(
        jnp.where(columns[None, :] == slot_other[:, None], logit_value, 0.0), axis=1
    )
    mixing = jax.nn.sigmoid(logit_value[:, 0] - partner_logit)
    return (jax.nn.silu(gate_value) * up_value * mixing[:, None]).astype(jnp.bfloat16)


def attention_kernel(offset_ref, q_ref, k_ref, v_ref, o_ref, *, per_shared, block_q, scale):
    seq = k_ref.shape[0]
    first = offset_ref[0] + pl.program_id(1) * block_q
    rows = first + lax.broadcasted_iota(jnp.int32, (block_q, seq), 0)
    cols = lax.broadcasted_iota(jnp.int32, (block_q, seq), 1)
    allowed = cols <= rows
    keys = k_ref[...]
    values = v_ref[...]
    for head in range(per_shared):
        query = q_ref[:, head * HEAD_SIZE : (head + 1) * HEAD_SIZE]
        scores = (
            lax.dot_general(
                query, keys, (((1,), (1,)), ((), ())), preferred_element_type=jnp.float32
            )
            * scale
        )
        masked = jnp.where(allowed, scores, NEG_FILL)
        row_max = jnp.max(masked, axis=1, keepdims=True)
        weights = jnp.exp(masked - row_max)
        total = jnp.sum(weights, axis=1, keepdims=True)
        acc = jnp.dot(weights.astype(jnp.bfloat16), values, preferred_element_type=jnp.float32)
        o_ref[:, head * HEAD_SIZE : (head + 1) * HEAD_SIZE] = (acc / total).astype(o_ref.dtype)


def attend(queries, packed_kv, offset, shared_heads, per_shared, interpret=False):
    rows_local = queries.shape[0]
    seq = packed_kv.shape[0]
    block_q = 256 if seq <= 2048 else 128
    block_q = min(block_q, rows_local)
    width = per_shared * HEAD_SIZE
    kernel = functools.partial(
        attention_kernel,
        per_shared=per_shared,
        block_q=block_q,
        scale=1.0 / math.sqrt(HEAD_SIZE),
    )
    grid_spec = pltpu.PrefetchScalarGridSpec(
        num_scalar_prefetch=1,
        grid=(shared_heads, rows_local // block_q),
        in_specs=[
            pl.BlockSpec((block_q, width), lambda g, b, off: (b, g)),
            pl.BlockSpec((seq, HEAD_SIZE), lambda g, b, off: (0, g)),
            pl.BlockSpec((seq, HEAD_SIZE), lambda g, b, off: (0, shared_heads + g)),
        ],
        out_specs=pl.BlockSpec((block_q, width), lambda g, b, off: (b, g)),
    )
    return pl.pallas_call(
        kernel,
        grid_spec=grid_spec,
        out_shape=jax.ShapeDtypeStruct((rows_local, shared_heads * width), jnp.bfloat16),
        compiler_params=pltpu.CompilerParams(vmem_limit_bytes=48 * 1024 * 1024),
        interpret=interpret,
    )(offset, queries, packed_kv, packed_kv)


def pair_exchange(x, axis, count, bit):
    return lax.ppermute(x, axis, perm=[(i, i ^ bit) for i in range(count)])


def gather_rows(x, axis):
    count = lax.axis_size(axis)
    if count & (count - 1):
        return lax.all_gather(x, axis, axis=0, tiled=True)
    index = lax.axis_index(axis)
    out = x
    bit = 1
    while bit < count:
        other = pair_exchange(out, axis, count, bit)
        upper = (index // bit) % 2
        size = out.shape[0]
        both = jnp.zeros((2 * size,) + out.shape[1:], out.dtype)
        both = lax.dynamic_update_slice_in_dim(both, out, upper * size, 0)
        out = lax.dynamic_update_slice_in_dim(both, other, (1 - upper) * size, 0)
        bit *= 2
    return out


def sum_rows(x, axis):
    count = lax.axis_size(axis)
    if count & (count - 1) or x.shape[0] % count:
        return lax.psum(x.astype(jnp.bfloat16), axis)
    index = lax.axis_index(axis)
    acc = x.astype(jnp.float32)
    bit = 1
    while bit < count:
        half = acc.shape[0] // 2
        upper = (index // bit) % 2
        keep = lax.dynamic_slice_in_dim(acc, upper * half, half, 0)
        send = lax.dynamic_slice_in_dim(acc, (1 - upper) * half, half, 0)
        other = pair_exchange(send.astype(jnp.bfloat16), axis, count, bit)
        acc = keep + other.astype(jnp.float32)
        bit *= 2
    out = acc.astype(jnp.bfloat16)
    bit = count // 2
    while bit >= 1:
        other = pair_exchange(out, axis, count, bit)
        upper = (index // bit) % 2
        size = out.shape[0]
        both = jnp.zeros((2 * size,) + out.shape[1:], out.dtype)
        both = lax.dynamic_update_slice_in_dim(both, out, upper * size, 0)
        out = lax.dynamic_update_slice_in_dim(both, other, (1 - upper) * size, 0)
        bit //= 2
    return out


def local(
    queries,
    key_rows,
    value_head_rows,
    residual,
    out_weight,
    norm_gain,
    router_weight,
    gate_weight,
    up_weight,
    down_weight,
    expert_ids,
    slot_ids,
):
    ctx_count = lax.axis_size("ctx")
    wide_index = lax.axis_index("wide")
    ctx_index = lax.axis_index("ctx")
    rows_local = queries.shape[0]
    heads_local = queries.shape[1] // HEAD_SIZE
    query_group_width = QUERY_HEADS // KEY_VALUE_HEADS
    shared_heads = max(1, heads_local // query_group_width)
    per_shared = heads_local // shared_heads
    first_shared = wide_index * heads_local // query_group_width
    key_used = lax.dynamic_slice_in_dim(
        key_rows, first_shared * HEAD_SIZE, shared_heads * HEAD_SIZE, 1
    )
    value_used = lax.dynamic_slice_in_dim(
        value_head_rows, first_shared * HEAD_SIZE, shared_heads * HEAD_SIZE, 1
    )
    packed_kv = gather_rows(jnp.concatenate([key_used, value_used], axis=1), "ctx")
    halves = 2 if rows_local % 256 == 0 else 1
    half_rows = rows_local // halves
    resid_parts = []
    for half in range(halves):
        offset = jnp.reshape(ctx_index * rows_local + half * half_rows, (1,)).astype(jnp.int32)
        query_part = lax.slice_in_dim(queries, half * half_rows, (half + 1) * half_rows, axis=0)
        attended = attend(query_part, packed_kv, offset, shared_heads, per_shared)
        partial_out = jnp.dot(attended, out_weight, preferred_element_type=jnp.float32)
        head_sum = lax.psum_scatter(
            partial_out.astype(jnp.bfloat16), "wide", scatter_dimension=1, tiled=True
        ).astype(jnp.float32)
        residual_part = lax.slice_in_dim(residual, half * half_rows, (half + 1) * half_rows, axis=0)
        resid_parts.append((residual_part.astype(jnp.float32) + head_sum).astype(jnp.bfloat16))
    resid = jnp.concatenate(resid_parts, axis=0)
    seq_len = rows_local * ctx_count
    capacity = seq_len * 5 // 16
    width_local = resid.shape[1]
    wide_count = lax.axis_size("wide")
    pieces = 2 if capacity % (16 * max(wide_count, ctx_count)) == 0 else 1
    piece_slots = capacity // pieces
    chunk = piece_slots // wide_count
    slot_of_token = token_slots(expert_ids, slot_ids, capacity)
    partner = jnp.sum(expert_ids, axis=1)
    slot_local = lax.dynamic_slice_in_dim(slot_of_token, ctx_index * rows_local, rows_local)
    gain = norm_gain.astype(jnp.float32)[None, :]
    moe_rows = jnp.zeros((rows_local, width_local), jnp.float32)
    after_sums = None
    after_down = None
    for piece in range(pieces):
        slot_ids_piece = piece * piece_slots + jnp.arange(piece_slots, dtype=jnp.int32)
        place = (slot_ids_piece[:, None] == slot_local[None, :]).astype(jnp.bfloat16)
        own_rows = jnp.dot(place, resid, preferred_element_type=jnp.float32)
        if after_sums is not None:
            own_rows, _ = lax.optimization_barrier((own_rows, after_sums))
        buffer = sum_rows(own_rows, "ctx")
        buffer_wide = buffer.astype(jnp.float32)
        square_part = jnp.sum(buffer_wide * buffer_wide, axis=1)
        scaled = (buffer_wide * gain).astype(jnp.bfloat16)
        gate_part = jnp.dot(scaled, gate_weight, preferred_element_type=jnp.float32)
        up_part = jnp.dot(scaled, up_weight, preferred_element_type=jnp.float32)
        logit_part = jnp.dot(scaled, router_weight, preferred_element_type=jnp.float32)
        experts = logit_part.shape[1]
        pad = 128 - (experts + 1) % 128
        small = jnp.concatenate(
            [logit_part, square_part[:, None], jnp.zeros((piece_slots, pad), jnp.float32)],
            axis=1,
        )
        sent = tuple(part.astype(jnp.bfloat16) for part in (gate_part, up_part, small))
        after_sums = sent
        gate_sum, up_sum, small_sum = (
            lax.psum_scatter(part, "wide", scatter_dimension=0, tiled=True).astype(jnp.float32)
            for part in sent
        )
        logit_sum = small_sum[:, :experts]
        square_sum = small_sum[:, experts]
        chunk_slots = piece * piece_slots + wide_index * chunk + jnp.arange(chunk, dtype=jnp.int32)
        other_chunk = jnp.sum(
            jnp.where(chunk_slots[:, None] == slot_of_token[None, :], partner[None, :], 0),
            axis=1,
        )
        hidden_chunk = expert_hidden(gate_sum, up_sum, square_sum, logit_sum, other_chunk, D)
        if after_down is not None:
            hidden_chunk, _ = lax.optimization_barrier((hidden_chunk, after_down))
        hidden = lax.all_gather(hidden_chunk, "wide", axis=0, tiled=True)
        expert_part = jnp.dot(hidden, down_weight, preferred_element_type=jnp.float32)
        after_down = expert_part
        expert_sum = sum_rows(expert_part, "ctx")
        pick = (slot_local[:, None] == slot_ids_piece[None, :]).astype(jnp.bfloat16)
        moe_rows = moe_rows + jnp.dot(pick, expert_sum, preferred_element_type=jnp.float32)
    return (resid.astype(jnp.float32) + moe_rows).astype(jnp.bfloat16)


def solution(mesh):
    placed = (
        P(("groups", "ctx"), "wide"),
        P(("groups", "ctx"), None),
        P(("groups", "ctx"), None),
        P(("groups", "ctx"), "wide"),
        P("wide", None),
        P("wide"),
        P("wide", None),
        P("wide", "ctx"),
        P("wide", "ctx"),
        P("ctx", "wide"),
        P("groups", None),
        P("groups", None),
    )
    return jax.shard_map(
        local, mesh=mesh, in_specs=placed, out_specs=P(("groups", "ctx"), "wide"), check_vma=False
    )
```

```python
import functools
import math

import jax
import jax.numpy as jnp
from jax import lax
from jax.experimental import pallas as pl
from jax.experimental.pallas import tpu as pltpu
from jax.sharding import PartitionSpec as P

D = 6144
QUERY_HEADS = 48
KEY_VALUE_HEADS = 8
HEAD_SIZE = 128


NEG_FILL = -1e30
EPSILON = 1e-05


def token_slots(expert_ids, slot_ids, capacity):
    in_window = jnp.logical_and(expert_ids == 0, slot_ids >= 0)
    picked = jnp.max(jnp.where(in_window, slot_ids, -1), axis=1)
    return jnp.where(picked >= 0, picked, capacity)


def other_experts(expert_ids, slot_of_token, capacity):
    partner = jnp.sum(expert_ids, axis=1)
    return jnp.zeros((capacity,), jnp.int32).at[slot_of_token].set(partner, mode="drop")


def expert_hidden(gate_sum, up_sum, square_sum, logit_sum, slot_other, model_width):
    inverse_rms = lax.rsqrt(square_sum / model_width + EPSILON)
    gate_value = gate_sum * inverse_rms[:, None]
    up_value = up_sum * inverse_rms[:, None]
    logit_value = logit_sum * inverse_rms[:, None]
    columns = jnp.arange(logit_value.shape[1], dtype=jnp.int32)
    partner_logit = jnp.sum(
        jnp.where(columns[None, :] == slot_other[:, None], logit_value, 0.0), axis=1
    )
    mixing = jax.nn.sigmoid(logit_value[:, 0] - partner_logit)
    return (jax.nn.silu(gate_value) * up_value * mixing[:, None]).astype(jnp.bfloat16)


def attention_kernel(offset_ref, q_ref, k_ref, v_ref, o_ref, *, per_shared, block_q, scale):
    seq = k_ref.shape[0]
    first = offset_ref[0] + pl.program_id(1) * block_q
    rows = first + lax.broadcasted_iota(jnp.int32, (block_q, seq), 0)
    cols = lax.broadcasted_iota(jnp.int32, (block_q, seq), 1)
    allowed = cols <= rows
    keys = k_ref[...]
    values = v_ref[...]
    for head in range(per_shared):
        query = q_ref[:, head * HEAD_SIZE : (head + 1) * HEAD_SIZE]
        scores = (
            lax.dot_general(
                query, keys, (((1,), (1,)), ((), ())), preferred_element_type=jnp.float32
            )
            * scale
        )
        masked = jnp.where(allowed, scores, NEG_FILL)
        row_max = jnp.max(masked, axis=1, keepdims=True)
        weights = jnp.exp(masked - row_max)
        total = jnp.sum(weights, axis=1, keepdims=True)
        acc = jnp.dot(weights.astype(jnp.bfloat16), values, preferred_element_type=jnp.float32)
        o_ref[:, head * HEAD_SIZE : (head + 1) * HEAD_SIZE] = (acc / total).astype(o_ref.dtype)


def attend(queries, packed_kv, offset, shared_heads, per_shared, interpret=False):
    rows_local = queries.shape[0]
    seq = packed_kv.shape[0]
    block_q = 256 if seq <= 2048 else 128
    block_q = min(block_q, rows_local)
    width = per_shared * HEAD_SIZE
    kernel = functools.partial(
        attention_kernel,
        per_shared=per_shared,
        block_q=block_q,
        scale=1.0 / math.sqrt(HEAD_SIZE),
    )
    grid_spec = pltpu.PrefetchScalarGridSpec(
        num_scalar_prefetch=1,
        grid=(shared_heads, rows_local // block_q),
        in_specs=[
            pl.BlockSpec((block_q, width), lambda g, b, off: (b, g)),
            pl.BlockSpec((seq, HEAD_SIZE), lambda g, b, off: (0, g)),
            pl.BlockSpec((seq, HEAD_SIZE), lambda g, b, off: (0, shared_heads + g)),
        ],
        out_specs=pl.BlockSpec((block_q, width), lambda g, b, off: (b, g)),
    )
    return pl.pallas_call(
        kernel,
        grid_spec=grid_spec,
        out_shape=jax.ShapeDtypeStruct((rows_local, shared_heads * width), jnp.bfloat16),
        compiler_params=pltpu.CompilerParams(vmem_limit_bytes=48 * 1024 * 1024),
        interpret=interpret,
    )(offset, queries, packed_kv, packed_kv)


def pair_exchange(x, axis, count, bit):
    return lax.ppermute(x, axis, perm=[(i, i ^ bit) for i in range(count)])


def gather_rows(x, axis):
    count = lax.axis_size(axis)
    if count & (count - 1):
        return lax.all_gather(x, axis, axis=0, tiled=True)
    index = lax.axis_index(axis)
    out = x
    bit = 1
    while bit < count:
        other = pair_exchange(out, axis, count, bit)
        upper = (index // bit) % 2
        size = out.shape[0]
        both = jnp.zeros((2 * size,) + out.shape[1:], out.dtype)
        both = lax.dynamic_update_slice_in_dim(both, out, upper * size, 0)
        out = lax.dynamic_update_slice_in_dim(both, other, (1 - upper) * size, 0)
        bit *= 2
    return out


def gather_causal(x, axis):
    count = lax.axis_size(axis)
    if count != 4:
        return gather_rows(x, axis)
    index = lax.axis_index(axis)
    rows = x.shape[0]
    lower = lax.ppermute(x, axis, perm=[(0, 2), (1, 3)])
    pair = jnp.concatenate([x, lower], axis=0)
    other = pair_exchange(pair, axis, count, 1)
    partner = index ^ 1
    out = jnp.zeros((count * rows,) + x.shape[1:], x.dtype)
    for block, at in (
        (x, index),
        (lower, (index + 2) % 4),
        (other[:rows], partner),
        (other[rows:], (partner + 2) % 4),
    ):
        out = lax.dynamic_update_slice_in_dim(out, block, at * rows, 0)
    return out


def sum_rows(x, axis):
    count = lax.axis_size(axis)
    if count & (count - 1) or x.shape[0] % count:
        return lax.psum(x.astype(jnp.bfloat16), axis)
    index = lax.axis_index(axis)
    acc = x.astype(jnp.float32)
    bit = 1
    while bit < count:
        half = acc.shape[0] // 2
        upper = (index // bit) % 2
        keep = lax.dynamic_slice_in_dim(acc, upper * half, half, 0)
        send = lax.dynamic_slice_in_dim(acc, (1 - upper) * half, half, 0)
        other = pair_exchange(send.astype(jnp.bfloat16), axis, count, bit)
        acc = keep + other.astype(jnp.float32)
        bit *= 2
    out = acc.astype(jnp.bfloat16)
    bit = count // 2
    while bit >= 1:
        other = pair_exchange(out, axis, count, bit)
        upper = (index // bit) % 2
        size = out.shape[0]
        both = jnp.zeros((2 * size,) + out.shape[1:], out.dtype)
        both = lax.dynamic_update_slice_in_dim(both, out, upper * size, 0)
        out = lax.dynamic_update_slice_in_dim(both, other, (1 - upper) * size, 0)
        bit //= 2
    return out


def local(
    queries,
    key_rows,
    value_head_rows,
    residual,
    out_weight,
    norm_gain,
    router_weight,
    gate_weight,
    up_weight,
    down_weight,
    expert_ids,
    slot_ids,
):
    ctx_count = lax.axis_size("ctx")
    wide_index = lax.axis_index("wide")
    ctx_index = lax.axis_index("ctx")
    rows_local = queries.shape[0]
    heads_local = queries.shape[1] // HEAD_SIZE
    query_group_width = QUERY_HEADS // KEY_VALUE_HEADS
    shared_heads = max(1, heads_local // query_group_width)
    per_shared = heads_local // shared_heads
    first_shared = wide_index * heads_local // query_group_width
    key_used = lax.dynamic_slice_in_dim(
        key_rows, first_shared * HEAD_SIZE, shared_heads * HEAD_SIZE, 1
    )
    value_used = lax.dynamic_slice_in_dim(
        value_head_rows, first_shared * HEAD_SIZE, shared_heads * HEAD_SIZE, 1
    )
    packed_kv = gather_causal(jnp.concatenate([key_used, value_used], axis=1), "ctx")
    offset = jnp.reshape(ctx_index * rows_local, (1,)).astype(jnp.int32)
    attended = attend(queries, packed_kv, offset, shared_heads, per_shared)
    partial_out = jnp.dot(attended, out_weight, preferred_element_type=jnp.float32)
    head_sum = lax.psum_scatter(
        partial_out.astype(jnp.bfloat16), "wide", scatter_dimension=1, tiled=True
    ).astype(jnp.float32)
    resid = (residual.astype(jnp.float32) + head_sum).astype(jnp.bfloat16)
    seq_len = rows_local * ctx_count
    capacity = seq_len * 5 // 16
    width_local = resid.shape[1]
    wide_count = lax.axis_size("wide")
    chunk = capacity // wide_count
    slot_of_token = token_slots(expert_ids, slot_ids, capacity)
    partner = jnp.sum(expert_ids, axis=1)
    slot_local = lax.dynamic_slice_in_dim(slot_of_token, ctx_index * rows_local, rows_local)
    slot_ids_all = jnp.arange(capacity, dtype=jnp.int32)
    place = (slot_ids_all[:, None] == slot_local[None, :]).astype(jnp.bfloat16)
    own_rows = jnp.dot(place, resid, preferred_element_type=jnp.float32)
    buffer = sum_rows(own_rows, "ctx")
    buffer_wide = buffer.astype(jnp.float32)
    square_part = jnp.sum(buffer_wide * buffer_wide, axis=1)
    scaled = (buffer_wide * norm_gain.astype(jnp.float32)[None, :]).astype(jnp.bfloat16)
    gate_part = jnp.dot(scaled, gate_weight, preferred_element_type=jnp.float32)
    up_part = jnp.dot(scaled, up_weight, preferred_element_type=jnp.float32)
    logit_part = jnp.dot(scaled, router_weight, preferred_element_type=jnp.float32)
    hidden_local = gate_part.shape[1]
    experts = logit_part.shape[1]
    pad = 128 - (experts + 1) % 128
    packed = jnp.concatenate(
        [
            gate_part,
            up_part,
            logit_part,
            square_part[:, None],
            jnp.zeros((capacity, pad), jnp.float32),
        ],
        axis=1,
    ).astype(jnp.bfloat16)
    reduced = lax.psum_scatter(packed, "wide", scatter_dimension=0, tiled=True).astype(
        jnp.float32
    )
    gate_sum = reduced[:, :hidden_local]
    up_sum = reduced[:, hidden_local : 2 * hidden_local]
    logit_sum = reduced[:, 2 * hidden_local : 2 * hidden_local + experts]
    square_sum = reduced[:, 2 * hidden_local + experts]
    chunk_slots = wide_index * chunk + jnp.arange(chunk, dtype=jnp.int32)
    other_chunk = jnp.sum(
        jnp.where(chunk_slots[:, None] == slot_of_token[None, :], partner[None, :], 0), axis=1
    )
    hidden_chunk = expert_hidden(gate_sum, up_sum, square_sum, logit_sum, other_chunk, D)
    hidden = lax.all_gather(hidden_chunk, "wide", axis=0, tiled=True)
    expert_part = jnp.dot(hidden, down_weight, preferred_element_type=jnp.float32)
    expert_sum = sum_rows(expert_part, "ctx")
    pick = (slot_local[:, None] == slot_ids_all[None, :]).astype(jnp.bfloat16)
    moe_rows = jnp.dot(pick, expert_sum, preferred_element_type=jnp.float32)
    return (resid.astype(jnp.float32) + moe_rows).astype(jnp.bfloat16)


def solution(mesh):
    placed = (
        P(("groups", "ctx"), "wide"),
        P(("groups", "ctx"), None),
        P(("groups", "ctx"), None),
        P(("groups", "ctx"), "wide"),
        P("wide", None),
        P("wide"),
        P("wide", None),
        P("wide", "ctx"),
        P("wide", "ctx"),
        P("ctx", "wide"),
        P("groups", None),
        P("groups", None),
    )
    return jax.shard_map(
        local, mesh=mesh, in_specs=placed, out_specs=P(("groups", "ctx"), "wide"), check_vma=False
    )
```

```python
import functools
import math

import jax
import jax.numpy as jnp
from jax import lax
from jax.experimental import pallas as pl
from jax.experimental.pallas import tpu as pltpu
from jax.sharding import PartitionSpec as P

D = 6144
QUERY_HEADS = 48
KEY_VALUE_HEADS = 8
HEAD_SIZE = 128


NEG_FILL = -1e30
EPSILON = 1e-05


def token_slots(expert_ids, slot_ids, capacity):
    in_window = jnp.logical_and(expert_ids == 0, slot_ids >= 0)
    picked = jnp.max(jnp.where(in_window, slot_ids, -1), axis=1)
    return jnp.where(picked >= 0, picked, capacity)


def other_experts(expert_ids, slot_of_token, capacity):
    partner = jnp.sum(expert_ids, axis=1)
    return jnp.zeros((capacity,), jnp.int32).at[slot_of_token].set(partner, mode="drop")


def expert_hidden(gate_sum, up_sum, square_sum, logit_sum, slot_other, model_width):
    inverse_rms = lax.rsqrt(square_sum / model_width + EPSILON)
    gate_value = gate_sum * inverse_rms[:, None]
    up_value = up_sum * inverse_rms[:, None]
    logit_value = logit_sum * inverse_rms[:, None]
    columns = jnp.arange(logit_value.shape[1], dtype=jnp.int32)
    partner_logit = jnp.sum(
        jnp.where(columns[None, :] == slot_other[:, None], logit_value, 0.0), axis=1
    )
    mixing = jax.nn.sigmoid(logit_value[:, 0] - partner_logit)
    return (jax.nn.silu(gate_value) * up_value * mixing[:, None]).astype(jnp.bfloat16)


def attention_kernel(offset_ref, q_ref, k_ref, v_ref, o_ref, *, per_shared, block_q, scale):
    seq = k_ref.shape[0]
    first = offset_ref[0] + pl.program_id(1) * block_q
    rows = first + lax.broadcasted_iota(jnp.int32, (block_q, seq), 0)
    cols = lax.broadcasted_iota(jnp.int32, (block_q, seq), 1)
    allowed = cols <= rows
    keys = k_ref[...]
    values = v_ref[...]
    for head in range(per_shared):
        query = q_ref[:, head * HEAD_SIZE : (head + 1) * HEAD_SIZE]
        scores = (
            lax.dot_general(
                query, keys, (((1,), (1,)), ((), ())), preferred_element_type=jnp.float32
            )
            * scale
        )
        masked = jnp.where(allowed, scores, NEG_FILL)
        row_max = jnp.max(masked, axis=1, keepdims=True)
        weights = jnp.exp(masked - row_max)
        total = jnp.sum(weights, axis=1, keepdims=True)
        acc = jnp.dot(weights.astype(jnp.bfloat16), values, preferred_element_type=jnp.float32)
        o_ref[:, head * HEAD_SIZE : (head + 1) * HEAD_SIZE] = (acc / total).astype(o_ref.dtype)


def attend(queries, packed_kv, offset, shared_heads, per_shared, interpret=False):
    rows_local = queries.shape[0]
    seq = packed_kv.shape[0]
    block_q = 256 if seq <= 2048 else 128
    block_q = min(block_q, rows_local)
    width = per_shared * HEAD_SIZE
    kernel = functools.partial(
        attention_kernel,
        per_shared=per_shared,
        block_q=block_q,
        scale=1.0 / math.sqrt(HEAD_SIZE),
    )
    grid_spec = pltpu.PrefetchScalarGridSpec(
        num_scalar_prefetch=1,
        grid=(shared_heads, rows_local // block_q),
        in_specs=[
            pl.BlockSpec((block_q, width), lambda g, b, off: (b, g)),
            pl.BlockSpec((seq, HEAD_SIZE), lambda g, b, off: (0, g)),
            pl.BlockSpec((seq, HEAD_SIZE), lambda g, b, off: (0, shared_heads + g)),
        ],
        out_specs=pl.BlockSpec((block_q, width), lambda g, b, off: (b, g)),
    )
    return pl.pallas_call(
        kernel,
        grid_spec=grid_spec,
        out_shape=jax.ShapeDtypeStruct((rows_local, shared_heads * width), jnp.bfloat16),
        compiler_params=pltpu.CompilerParams(vmem_limit_bytes=48 * 1024 * 1024),
        interpret=interpret,
    )(offset, queries, packed_kv, packed_kv)


def pair_exchange(x, axis, count, bit):
    return lax.ppermute(x, axis, perm=[(i, i ^ bit) for i in range(count)])


def gather_rows(x, axis):
    count = lax.axis_size(axis)
    if count & (count - 1):
        return lax.all_gather(x, axis, axis=0, tiled=True)
    index = lax.axis_index(axis)
    out = x
    bit = 1
    while bit < count:
        other = pair_exchange(out, axis, count, bit)
        upper = (index // bit) % 2
        size = out.shape[0]
        both = jnp.zeros((2 * size,) + out.shape[1:], out.dtype)
        both = lax.dynamic_update_slice_in_dim(both, out, upper * size, 0)
        out = lax.dynamic_update_slice_in_dim(both, other, (1 - upper) * size, 0)
        bit *= 2
    return out


def gather_causal(x, axis):
    count = lax.axis_size(axis)
    if count != 4:
        return gather_rows(x, axis)
    index = lax.axis_index(axis)
    rows = x.shape[0]
    lower = lax.ppermute(x, axis, perm=[(0, 2), (1, 3)])
    pair = jnp.concatenate([x, lower], axis=0)
    other = pair_exchange(pair, axis, count, 1)
    partner = index ^ 1
    out = jnp.zeros((count * rows,) + x.shape[1:], x.dtype)
    for block, at in (
        (x, index),
        (lower, (index + 2) % 4),
        (other[:rows], partner),
        (other[rows:], (partner + 2) % 4),
    ):
        out = lax.dynamic_update_slice_in_dim(out, block, at * rows, 0)
    return out


def sum_rows(x, axis):
    count = lax.axis_size(axis)
    if count & (count - 1) or x.shape[0] % count:
        return lax.psum(x.astype(jnp.bfloat16), axis)
    index = lax.axis_index(axis)
    acc = x.astype(jnp.float32)
    bit = 1
    while bit < count:
        half = acc.shape[0] // 2
        upper = (index // bit) % 2
        keep = lax.dynamic_slice_in_dim(acc, upper * half, half, 0)
        send = lax.dynamic_slice_in_dim(acc, (1 - upper) * half, half, 0)
        other = pair_exchange(send.astype(jnp.bfloat16), axis, count, bit)
        acc = keep + other.astype(jnp.float32)
        bit *= 2
    out = acc.astype(jnp.bfloat16)
    bit = count // 2
    while bit >= 1:
        other = pair_exchange(out, axis, count, bit)
        upper = (index // bit) % 2
        size = out.shape[0]
        both = jnp.zeros((2 * size,) + out.shape[1:], out.dtype)
        both = lax.dynamic_update_slice_in_dim(both, out, upper * size, 0)
        out = lax.dynamic_update_slice_in_dim(both, other, (1 - upper) * size, 0)
        bit //= 2
    return out


def local(
    queries,
    key_rows,
    value_head_rows,
    residual,
    out_weight,
    norm_gain,
    router_weight,
    gate_weight,
    up_weight,
    down_weight,
    expert_ids,
    slot_ids,
):
    ctx_count = lax.axis_size("ctx")
    wide_index = lax.axis_index("wide")
    ctx_index = lax.axis_index("ctx")
    rows_local = queries.shape[0]
    heads_local = queries.shape[1] // HEAD_SIZE
    query_group_width = QUERY_HEADS // KEY_VALUE_HEADS
    shared_heads = max(1, heads_local // query_group_width)
    per_shared = heads_local // shared_heads
    first_shared = wide_index * heads_local // query_group_width
    key_used = lax.dynamic_slice_in_dim(
        key_rows, first_shared * HEAD_SIZE, shared_heads * HEAD_SIZE, 1
    )
    value_used = lax.dynamic_slice_in_dim(
        value_head_rows, first_shared * HEAD_SIZE, shared_heads * HEAD_SIZE, 1
    )
    packed_kv = gather_causal(jnp.concatenate([key_used, value_used], axis=1), "ctx")
    offset = jnp.reshape(ctx_index * rows_local, (1,)).astype(jnp.int32)
    attended = attend(queries, packed_kv, offset, shared_heads, per_shared)
    partial_out = jnp.dot(attended, out_weight, preferred_element_type=jnp.float32)
    head_sum = lax.psum_scatter(
        partial_out.astype(jnp.bfloat16), "wide", scatter_dimension=1, tiled=True
    ).astype(jnp.float32)
    resid = (residual.astype(jnp.float32) + head_sum).astype(jnp.bfloat16)
    seq_len = rows_local * ctx_count
    capacity = seq_len * 5 // 16
    width_local = resid.shape[1]
    wide_count = lax.axis_size("wide")
    slot_of_token = token_slots(expert_ids, slot_ids, capacity)
    partner = jnp.sum(expert_ids, axis=1)
    slot_local = lax.dynamic_slice_in_dim(slot_of_token, ctx_index * rows_local, rows_local)
    pieces = 2 if capacity % (16 * max(wide_count, ctx_count)) == 0 else 1
    piece_slots = capacity // pieces
    chunk = piece_slots // wide_count
    gain = norm_gain.astype(jnp.float32)[None, :]
    moe_rows = jnp.zeros((rows_local, width_local), jnp.float32)
    after_sums = None
    after_down = None
    for piece in range(pieces):
        slot_ids_piece = piece * piece_slots + jnp.arange(piece_slots, dtype=jnp.int32)
        place = (slot_ids_piece[:, None] == slot_local[None, :]).astype(jnp.bfloat16)
        own_rows = jnp.dot(place, resid, preferred_element_type=jnp.float32)
        if after_sums is not None:
            own_rows, _ = lax.optimization_barrier((own_rows, after_sums))
        buffer = sum_rows(own_rows, "ctx")
        buffer_wide = buffer.astype(jnp.float32)
        square_part = jnp.sum(buffer_wide * buffer_wide, axis=1)
        scaled = (buffer_wide * gain).astype(jnp.bfloat16)
        gate_part = jnp.dot(scaled, gate_weight, preferred_element_type=jnp.float32)
        up_part = jnp.dot(scaled, up_weight, preferred_element_type=jnp.float32)
        logit_part = jnp.dot(scaled, router_weight, preferred_element_type=jnp.float32)
        hidden_local = gate_part.shape[1]
        experts = logit_part.shape[1]
        pad = 128 - (experts + 1) % 128
        packed = jnp.concatenate(
            [
                gate_part,
                up_part,
                logit_part,
                square_part[:, None],
                jnp.zeros((piece_slots, pad), jnp.float32),
            ],
            axis=1,
        ).astype(jnp.bfloat16)
        after_sums = packed
        reduced = lax.psum_scatter(packed, "wide", scatter_dimension=0, tiled=True).astype(
            jnp.float32
        )
        gate_sum = reduced[:, :hidden_local]
        up_sum = reduced[:, hidden_local : 2 * hidden_local]
        logit_sum = reduced[:, 2 * hidden_local : 2 * hidden_local + experts]
        square_sum = reduced[:, 2 * hidden_local + experts]
        chunk_slots = piece * piece_slots + wide_index * chunk + jnp.arange(chunk, dtype=jnp.int32)
        other_chunk = jnp.sum(
            jnp.where(chunk_slots[:, None] == slot_of_token[None, :], partner[None, :], 0),
            axis=1,
        )
        hidden_chunk = expert_hidden(gate_sum, up_sum, square_sum, logit_sum, other_chunk, D)
        if after_down is not None:
            hidden_chunk, _ = lax.optimization_barrier((hidden_chunk, after_down))
        hidden = lax.all_gather(hidden_chunk, "wide", axis=0, tiled=True)
        expert_part = jnp.dot(hidden, down_weight, preferred_element_type=jnp.float32)
        after_down = expert_part
        expert_sum = sum_rows(expert_part, "ctx")
        pick = (slot_local[:, None] == slot_ids_piece[None, :]).astype(jnp.bfloat16)
        moe_rows = moe_rows + jnp.dot(pick, expert_sum, preferred_element_type=jnp.float32)
    return (resid.astype(jnp.float32) + moe_rows).astype(jnp.bfloat16)


def solution(mesh):
    placed = (
        P(("groups", "ctx"), "wide"),
        P(("groups", "ctx"), None),
        P(("groups", "ctx"), None),
        P(("groups", "ctx"), "wide"),
        P("wide", None),
        P("wide"),
        P("wide", None),
        P("wide", "ctx"),
        P("wide", "ctx"),
        P("ctx", "wide"),
        P("groups", None),
        P("groups", None),
    )
    return jax.shard_map(
        local, mesh=mesh, in_specs=placed, out_specs=P(("groups", "ctx"), "wide"), check_vma=False
    )
```

```python
import functools
import math

import jax
import jax.numpy as jnp
from jax import lax
from jax.experimental import pallas as pl
from jax.experimental.pallas import tpu as pltpu
from jax.sharding import PartitionSpec as P

D = 6144
QUERY_HEADS = 48
KEY_VALUE_HEADS = 8
HEAD_SIZE = 128


NEG_FILL = -1e30
EPSILON = 1e-05


def token_slots(expert_ids, slot_ids, capacity):
    in_window = jnp.logical_and(expert_ids == 0, slot_ids >= 0)
    picked = jnp.max(jnp.where(in_window, slot_ids, -1), axis=1)
    return jnp.where(picked >= 0, picked, capacity)


def other_experts(expert_ids, slot_of_token, capacity):
    partner = jnp.sum(expert_ids, axis=1)
    return jnp.zeros((capacity,), jnp.int32).at[slot_of_token].set(partner, mode="drop")


def expert_hidden(gate_sum, up_sum, square_sum, logit_sum, slot_other, model_width):
    inverse_rms = lax.rsqrt(square_sum / model_width + EPSILON)
    gate_value = gate_sum * inverse_rms[:, None]
    up_value = up_sum * inverse_rms[:, None]
    logit_value = logit_sum * inverse_rms[:, None]
    columns = jnp.arange(logit_value.shape[1], dtype=jnp.int32)
    partner_logit = jnp.sum(
        jnp.where(columns[None, :] == slot_other[:, None], logit_value, 0.0), axis=1
    )
    mixing = jax.nn.sigmoid(logit_value[:, 0] - partner_logit)
    return (jax.nn.silu(gate_value) * up_value * mixing[:, None]).astype(jnp.bfloat16)


def attention_kernel(offset_ref, q_ref, k_ref, v_ref, o_ref, *, per_shared, block_q, scale):
    seq = k_ref.shape[0]
    first = offset_ref[0] + pl.program_id(1) * block_q
    rows = first + lax.broadcasted_iota(jnp.int32, (block_q, seq), 0)
    cols = lax.broadcasted_iota(jnp.int32, (block_q, seq), 1)
    allowed = cols <= rows
    keys = k_ref[...]
    values = v_ref[...]
    for head in range(per_shared):
        query = q_ref[:, head * HEAD_SIZE : (head + 1) * HEAD_SIZE]
        scores = (
            lax.dot_general(
                query, keys, (((1,), (1,)), ((), ())), preferred_element_type=jnp.float32
            )
            * scale
        )
        masked = jnp.where(allowed, scores, NEG_FILL)
        row_max = jnp.max(masked, axis=1, keepdims=True)
        weights = jnp.exp(masked - row_max)
        total = jnp.sum(weights, axis=1, keepdims=True)
        acc = jnp.dot(weights.astype(jnp.bfloat16), values, preferred_element_type=jnp.float32)
        o_ref[:, head * HEAD_SIZE : (head + 1) * HEAD_SIZE] = (acc / total).astype(o_ref.dtype)


def attend(queries, packed_kv, offset, shared_heads, per_shared, interpret=False):
    rows_local = queries.shape[0]
    seq = packed_kv.shape[0]
    block_q = 256 if seq <= 2048 else 128
    block_q = min(block_q, rows_local)
    width = per_shared * HEAD_SIZE
    kernel = functools.partial(
        attention_kernel,
        per_shared=per_shared,
        block_q=block_q,
        scale=1.0 / math.sqrt(HEAD_SIZE),
    )
    grid_spec = pltpu.PrefetchScalarGridSpec(
        num_scalar_prefetch=1,
        grid=(shared_heads, rows_local // block_q),
        in_specs=[
            pl.BlockSpec((block_q, width), lambda g, b, off: (b, g)),
            pl.BlockSpec((seq, HEAD_SIZE), lambda g, b, off: (0, g)),
            pl.BlockSpec((seq, HEAD_SIZE), lambda g, b, off: (0, shared_heads + g)),
        ],
        out_specs=pl.BlockSpec((block_q, width), lambda g, b, off: (b, g)),
    )
    return pl.pallas_call(
        kernel,
        grid_spec=grid_spec,
        out_shape=jax.ShapeDtypeStruct((rows_local, shared_heads * width), jnp.bfloat16),
        compiler_params=pltpu.CompilerParams(vmem_limit_bytes=48 * 1024 * 1024),
        interpret=interpret,
    )(offset, queries, packed_kv, packed_kv)


def pair_exchange(x, axis, count, bit):
    return lax.ppermute(x, axis, perm=[(i, i ^ bit) for i in range(count)])


def gather_rows(x, axis):
    count = lax.axis_size(axis)
    if count & (count - 1):
        return lax.all_gather(x, axis, axis=0, tiled=True)
    index = lax.axis_index(axis)
    out = x
    bit = 1
    while bit < count:
        other = pair_exchange(out, axis, count, bit)
        upper = (index // bit) % 2
        size = out.shape[0]
        both = jnp.zeros((2 * size,) + out.shape[1:], out.dtype)
        both = lax.dynamic_update_slice_in_dim(both, out, upper * size, 0)
        out = lax.dynamic_update_slice_in_dim(both, other, (1 - upper) * size, 0)
        bit *= 2
    return out


def gather_causal(x, axis):
    count = lax.axis_size(axis)
    if count != 4:
        return gather_rows(x, axis)
    index = lax.axis_index(axis)
    rows = x.shape[0]
    lower = lax.ppermute(x, axis, perm=[(0, 2), (1, 3)])
    pair = jnp.concatenate([x, lower], axis=0)
    other = pair_exchange(pair, axis, count, 1)
    partner = index ^ 1
    out = jnp.zeros((count * rows,) + x.shape[1:], x.dtype)
    for block, at in (
        (x, index),
        (lower, (index + 2) % 4),
        (other[:rows], partner),
        (other[rows:], (partner + 2) % 4),
    ):
        out = lax.dynamic_update_slice_in_dim(out, block, at * rows, 0)
    return out


def sum_rows(x, axis):
    count = lax.axis_size(axis)
    if count & (count - 1) or x.shape[0] % count:
        return lax.psum(x.astype(jnp.bfloat16), axis)
    index = lax.axis_index(axis)
    acc = x.astype(jnp.float32)
    bit = 1
    while bit < count:
        half = acc.shape[0] // 2
        upper = (index // bit) % 2
        keep = lax.dynamic_slice_in_dim(acc, upper * half, half, 0)
        send = lax.dynamic_slice_in_dim(acc, (1 - upper) * half, half, 0)
        other = pair_exchange(send.astype(jnp.bfloat16), axis, count, bit)
        acc = keep + other.astype(jnp.float32)
        bit *= 2
    out = acc.astype(jnp.bfloat16)
    bit = count // 2
    while bit >= 1:
        other = pair_exchange(out, axis, count, bit)
        upper = (index // bit) % 2
        size = out.shape[0]
        both = jnp.zeros((2 * size,) + out.shape[1:], out.dtype)
        both = lax.dynamic_update_slice_in_dim(both, out, upper * size, 0)
        out = lax.dynamic_update_slice_in_dim(both, other, (1 - upper) * size, 0)
        bit //= 2
    return out


def local(
    queries,
    key_rows,
    value_head_rows,
    residual,
    out_weight,
    norm_gain,
    router_weight,
    gate_weight,
    up_weight,
    down_weight,
    expert_ids,
    slot_ids,
):
    ctx_count = lax.axis_size("ctx")
    wide_index = lax.axis_index("wide")
    ctx_index = lax.axis_index("ctx")
    rows_local = queries.shape[0]
    heads_local = queries.shape[1] // HEAD_SIZE
    query_group_width = QUERY_HEADS // KEY_VALUE_HEADS
    shared_heads = max(1, heads_local // query_group_width)
    per_shared = heads_local // shared_heads
    first_shared = wide_index * heads_local // query_group_width
    key_used = lax.dynamic_slice_in_dim(
        key_rows, first_shared * HEAD_SIZE, shared_heads * HEAD_SIZE, 1
    )
    value_used = lax.dynamic_slice_in_dim(
        value_head_rows, first_shared * HEAD_SIZE, shared_heads * HEAD_SIZE, 1
    )
    packed_kv = gather_causal(jnp.concatenate([key_used, value_used], axis=1), "ctx")
    offset = jnp.reshape(ctx_index * rows_local, (1,)).astype(jnp.int32)
    attended = attend(queries, packed_kv, offset, shared_heads, per_shared)
    partial_out = jnp.dot(attended, out_weight, preferred_element_type=jnp.float32)
    head_sum = lax.psum_scatter(
        partial_out.astype(jnp.bfloat16), "wide", scatter_dimension=1, tiled=True
    ).astype(jnp.float32)
    resid = (residual.astype(jnp.float32) + head_sum).astype(jnp.bfloat16)
    seq_len = rows_local * ctx_count
    capacity = seq_len * 5 // 16
    width_local = resid.shape[1]
    wide_count = lax.axis_size("wide")
    chunk = capacity // wide_count
    slot_of_token = token_slots(expert_ids, slot_ids, capacity)
    partner = jnp.sum(expert_ids, axis=1)
    slot_local = lax.dynamic_slice_in_dim(slot_of_token, ctx_index * rows_local, rows_local)
    slot_ids_all = jnp.arange(capacity, dtype=jnp.int32)
    place = (slot_ids_all[:, None] == slot_local[None, :]).astype(jnp.bfloat16)
    own_rows = jnp.dot(place, resid, preferred_element_type=jnp.float32)
    buffer = sum_rows(own_rows, "ctx")
    buffer_wide = buffer.astype(jnp.float32)
    square_part = jnp.sum(buffer_wide * buffer_wide, axis=1)
    scaled = (buffer_wide * norm_gain.astype(jnp.float32)[None, :]).astype(jnp.bfloat16)
    both_part = jnp.dot(
        scaled,
        jnp.concatenate([gate_weight, up_weight], axis=1),
        preferred_element_type=jnp.float32,
    )
    logit_part = jnp.dot(scaled, router_weight, preferred_element_type=jnp.float32)
    hidden_local = gate_weight.shape[1]
    experts = logit_part.shape[1]
    pad = 128 - (experts + 1) % 128
    small = jnp.concatenate(
        [logit_part, square_part[:, None], jnp.zeros((capacity, pad), jnp.float32)], axis=1
    )
    both_sum, small_sum = (
        lax.psum_scatter(part.astype(jnp.bfloat16), "wide", scatter_dimension=0, tiled=True)
        .astype(jnp.float32)
        for part in (both_part, small)
    )
    gate_sum = both_sum[:, :hidden_local]
    up_sum = both_sum[:, hidden_local:]
    logit_sum = small_sum[:, :experts]
    square_sum = small_sum[:, experts]
    chunk_slots = wide_index * chunk + jnp.arange(chunk, dtype=jnp.int32)
    other_chunk = jnp.sum(
        jnp.where(chunk_slots[:, None] == slot_of_token[None, :], partner[None, :], 0), axis=1
    )
    hidden_chunk = expert_hidden(gate_sum, up_sum, square_sum, logit_sum, other_chunk, D)
    hidden = lax.all_gather(hidden_chunk, "wide", axis=0, tiled=True)
    expert_part = jnp.dot(hidden, down_weight, preferred_element_type=jnp.float32)
    expert_sum = sum_rows(expert_part, "ctx")
    pick = (slot_local[:, None] == slot_ids_all[None, :]).astype(jnp.bfloat16)
    moe_rows = jnp.dot(pick, expert_sum, preferred_element_type=jnp.float32)
    return (resid.astype(jnp.float32) + moe_rows).astype(jnp.bfloat16)


def solution(mesh):
    placed = (
        P(("groups", "ctx"), "wide"),
        P(("groups", "ctx"), None),
        P(("groups", "ctx"), None),
        P(("groups", "ctx"), "wide"),
        P("wide", None),
        P("wide"),
        P("wide", None),
        P("wide", "ctx"),
        P("wide", "ctx"),
        P("ctx", "wide"),
        P("groups", None),
        P("groups", None),
    )
    return jax.shard_map(
        local, mesh=mesh, in_specs=placed, out_specs=P(("groups", "ctx"), "wide"), check_vma=False
    )
```

```python
import functools
import math

import jax
import jax.numpy as jnp
from jax import lax
from jax.experimental import pallas as pl
from jax.experimental.pallas import tpu as pltpu
from jax.sharding import PartitionSpec as P

D = 6144
QUERY_HEADS = 48
KEY_VALUE_HEADS = 8
HEAD_SIZE = 128


NEG_FILL = -1e30
EPSILON = 1e-05


def token_slots(expert_ids, slot_ids, capacity):
    in_window = jnp.logical_and(expert_ids == 0, slot_ids >= 0)
    picked = jnp.max(jnp.where(in_window, slot_ids, -1), axis=1)
    return jnp.where(picked >= 0, picked, capacity)


def other_experts(expert_ids, slot_of_token, capacity):
    partner = jnp.sum(expert_ids, axis=1)
    return jnp.zeros((capacity,), jnp.int32).at[slot_of_token].set(partner, mode="drop")


def expert_hidden(gate_sum, up_sum, square_sum, logit_sum, slot_other, model_width):
    inverse_rms = lax.rsqrt(square_sum / model_width + EPSILON)
    gate_value = gate_sum * inverse_rms[:, None]
    up_value = up_sum * inverse_rms[:, None]
    logit_value = logit_sum * inverse_rms[:, None]
    columns = jnp.arange(logit_value.shape[1], dtype=jnp.int32)
    partner_logit = jnp.sum(
        jnp.where(columns[None, :] == slot_other[:, None], logit_value, 0.0), axis=1
    )
    mixing = jax.nn.sigmoid(logit_value[:, 0] - partner_logit)
    return (jax.nn.silu(gate_value) * up_value * mixing[:, None]).astype(jnp.bfloat16)


def attention_kernel(offset_ref, q_ref, k_ref, v_ref, o_ref, *, per_shared, block_q, scale):
    seq = k_ref.shape[0]
    first = offset_ref[0] + pl.program_id(1) * block_q
    rows = first + lax.broadcasted_iota(jnp.int32, (block_q, seq), 0)
    cols = lax.broadcasted_iota(jnp.int32, (block_q, seq), 1)
    allowed = cols <= rows
    keys = k_ref[...]
    values = v_ref[...]
    for head in range(per_shared):
        query = q_ref[:, head * HEAD_SIZE : (head + 1) * HEAD_SIZE]
        scores = (
            lax.dot_general(
                query, keys, (((1,), (1,)), ((), ())), preferred_element_type=jnp.float32
            )
            * scale
        )
        masked = jnp.where(allowed, scores, NEG_FILL)
        row_max = jnp.max(masked, axis=1, keepdims=True)
        weights = jnp.exp(masked - row_max)
        total = jnp.sum(weights, axis=1, keepdims=True)
        acc = jnp.dot(weights.astype(jnp.bfloat16), values, preferred_element_type=jnp.float32)
        o_ref[:, head * HEAD_SIZE : (head + 1) * HEAD_SIZE] = (acc / total).astype(o_ref.dtype)


def attend(queries, packed_kv, offset, shared_heads, per_shared, interpret=False):
    rows_local = queries.shape[0]
    seq = packed_kv.shape[0]
    block_q = 256 if seq <= 2048 else 128
    block_q = min(block_q, rows_local)
    width = per_shared * HEAD_SIZE
    kernel = functools.partial(
        attention_kernel,
        per_shared=per_shared,
        block_q=block_q,
        scale=1.0 / math.sqrt(HEAD_SIZE),
    )
    grid_spec = pltpu.PrefetchScalarGridSpec(
        num_scalar_prefetch=1,
        grid=(shared_heads, rows_local // block_q),
        in_specs=[
            pl.BlockSpec((block_q, width), lambda g, b, off: (b, g)),
            pl.BlockSpec((seq, HEAD_SIZE), lambda g, b, off: (0, g)),
            pl.BlockSpec((seq, HEAD_SIZE), lambda g, b, off: (0, shared_heads + g)),
        ],
        out_specs=pl.BlockSpec((block_q, width), lambda g, b, off: (b, g)),
    )
    return pl.pallas_call(
        kernel,
        grid_spec=grid_spec,
        out_shape=jax.ShapeDtypeStruct((rows_local, shared_heads * width), jnp.bfloat16),
        compiler_params=pltpu.CompilerParams(vmem_limit_bytes=48 * 1024 * 1024),
        interpret=interpret,
    )(offset, queries, packed_kv, packed_kv)


def pair_exchange(x, axis, count, bit):
    return lax.ppermute(x, axis, perm=[(i, i ^ bit) for i in range(count)])


def gather_rows(x, axis):
    count = lax.axis_size(axis)
    if count & (count - 1):
        return lax.all_gather(x, axis, axis=0, tiled=True)
    index = lax.axis_index(axis)
    out = x
    bit = 1
    while bit < count:
        other = pair_exchange(out, axis, count, bit)
        upper = (index // bit) % 2
        size = out.shape[0]
        both = jnp.zeros((2 * size,) + out.shape[1:], out.dtype)
        both = lax.dynamic_update_slice_in_dim(both, out, upper * size, 0)
        out = lax.dynamic_update_slice_in_dim(both, other, (1 - upper) * size, 0)
        bit *= 2
    return out


def gather_causal(x, axis):
    count = lax.axis_size(axis)
    if count != 4:
        return gather_rows(x, axis)
    index = lax.axis_index(axis)
    rows = x.shape[0]
    lower = lax.ppermute(x, axis, perm=[(0, 2), (1, 3)])
    pair = jnp.concatenate([x, lower], axis=0)
    other = pair_exchange(pair, axis, count, 1)
    partner = index ^ 1
    out = jnp.zeros((count * rows,) + x.shape[1:], x.dtype)
    for block, at in (
        (x, index),
        (lower, (index + 2) % 4),
        (other[:rows], partner),
        (other[rows:], (partner + 2) % 4),
    ):
        out = lax.dynamic_update_slice_in_dim(out, block, at * rows, 0)
    return out


def sum_rows(x, axis):
    count = lax.axis_size(axis)
    if count & (count - 1) or x.shape[0] % count:
        return lax.psum(x.astype(jnp.bfloat16), axis)
    index = lax.axis_index(axis)
    acc = x.astype(jnp.float32)
    bit = 1
    while bit < count:
        half = acc.shape[0] // 2
        upper = (index // bit) % 2
        keep = lax.dynamic_slice_in_dim(acc, upper * half, half, 0)
        send = lax.dynamic_slice_in_dim(acc, (1 - upper) * half, half, 0)
        other = pair_exchange(send.astype(jnp.bfloat16), axis, count, bit)
        acc = keep + other.astype(jnp.float32)
        bit *= 2
    out = acc.astype(jnp.bfloat16)
    bit = count // 2
    while bit >= 1:
        other = pair_exchange(out, axis, count, bit)
        upper = (index // bit) % 2
        size = out.shape[0]
        both = jnp.zeros((2 * size,) + out.shape[1:], out.dtype)
        both = lax.dynamic_update_slice_in_dim(both, out, upper * size, 0)
        out = lax.dynamic_update_slice_in_dim(both, other, (1 - upper) * size, 0)
        bit //= 2
    return out


def local(
    queries,
    key_rows,
    value_head_rows,
    residual,
    out_weight,
    norm_gain,
    router_weight,
    gate_weight,
    up_weight,
    down_weight,
    expert_ids,
    slot_ids,
):
    ctx_count = lax.axis_size("ctx")
    wide_index = lax.axis_index("wide")
    ctx_index = lax.axis_index("ctx")
    rows_local = queries.shape[0]
    heads_local = queries.shape[1] // HEAD_SIZE
    query_group_width = QUERY_HEADS // KEY_VALUE_HEADS
    shared_heads = max(1, heads_local // query_group_width)
    per_shared = heads_local // shared_heads
    first_shared = wide_index * heads_local // query_group_width
    key_used = lax.dynamic_slice_in_dim(
        key_rows, first_shared * HEAD_SIZE, shared_heads * HEAD_SIZE, 1
    )
    value_used = lax.dynamic_slice_in_dim(
        value_head_rows, first_shared * HEAD_SIZE, shared_heads * HEAD_SIZE, 1
    )
    packed_kv = gather_causal(jnp.concatenate([key_used, value_used], axis=1), "ctx")
    offset = jnp.reshape(ctx_index * rows_local, (1,)).astype(jnp.int32)
    attended = attend(queries, packed_kv, offset, shared_heads, per_shared)
    partial_out = jnp.dot(attended, out_weight, preferred_element_type=jnp.float32)
    head_sum = lax.psum_scatter(
        partial_out.astype(jnp.bfloat16), "wide", scatter_dimension=1, tiled=True
    ).astype(jnp.float32)
    resid = (residual.astype(jnp.float32) + head_sum).astype(jnp.bfloat16)
    seq_len = rows_local * ctx_count
    capacity = seq_len * 5 // 16
    width_local = resid.shape[1]
    wide_count = lax.axis_size("wide")
    chunk = capacity // wide_count
    slot_of_token = token_slots(expert_ids, slot_ids, capacity)
    partner = jnp.sum(expert_ids, axis=1)
    slot_local = lax.dynamic_slice_in_dim(slot_of_token, ctx_index * rows_local, rows_local)
    slot_ids_all = jnp.arange(capacity, dtype=jnp.int32)
    place = (slot_ids_all[:, None] == slot_local[None, :]).astype(jnp.bfloat16)
    own_rows = jnp.dot(place, resid, preferred_element_type=jnp.float32)
    buffer = sum_rows(own_rows, "ctx")
    buffer_wide = buffer.astype(jnp.float32)
    square_part = jnp.sum(buffer_wide * buffer_wide, axis=1)
    scaled = (buffer_wide * norm_gain.astype(jnp.float32)[None, :]).astype(jnp.bfloat16)
    both_part = jnp.dot(
        scaled,
        jnp.concatenate([gate_weight, up_weight], axis=1),
        preferred_element_type=jnp.float32,
    )
    logit_part = jnp.dot(scaled, router_weight, preferred_element_type=jnp.float32)
    hidden_local = gate_weight.shape[1]
    experts = logit_part.shape[1]
    pad = 128 - (experts + 1) % 128
    small = jnp.concatenate(
        [logit_part, square_part[:, None], jnp.zeros((capacity, pad), jnp.float32)], axis=1
    )
    both_sum = lax.psum_scatter(
        both_part.astype(jnp.bfloat16), "wide", scatter_dimension=0, tiled=True
    ).astype(jnp.float32)
    small_sum = lax.dynamic_slice_in_dim(
        sum_rows(small, "wide"), wide_index * chunk, chunk, 0
    ).astype(jnp.float32)
    gate_sum = both_sum[:, :hidden_local]
    up_sum = both_sum[:, hidden_local:]
    logit_sum = small_sum[:, :experts]
    square_sum = small_sum[:, experts]
    chunk_slots = wide_index * chunk + jnp.arange(chunk, dtype=jnp.int32)
    other_chunk = jnp.sum(
        jnp.where(chunk_slots[:, None] == slot_of_token[None, :], partner[None, :], 0), axis=1
    )
    hidden_chunk = expert_hidden(gate_sum, up_sum, square_sum, logit_sum, other_chunk, D)
    hidden = lax.all_gather(hidden_chunk, "wide", axis=0, tiled=True)
    expert_part = jnp.dot(hidden, down_weight, preferred_element_type=jnp.float32)
    expert_sum = sum_rows(expert_part, "ctx")
    pick = (slot_local[:, None] == slot_ids_all[None, :]).astype(jnp.bfloat16)
    moe_rows = jnp.dot(pick, expert_sum, preferred_element_type=jnp.float32)
    return (resid.astype(jnp.float32) + moe_rows).astype(jnp.bfloat16)


def solution(mesh):
    placed = (
        P(("groups", "ctx"), "wide"),
        P(("groups", "ctx"), None),
        P(("groups", "ctx"), None),
        P(("groups", "ctx"), "wide"),
        P("wide", None),
        P("wide"),
        P("wide", None),
        P("wide", "ctx"),
        P("wide", "ctx"),
        P("ctx", "wide"),
        P("groups", None),
        P("groups", None),
    )
    return jax.shard_map(
        local, mesh=mesh, in_specs=placed, out_specs=P(("groups", "ctx"), "wide"), check_vma=False
    )
```

```python
import functools
import math

import jax
import jax.numpy as jnp
from jax import lax
from jax.experimental import pallas as pl
from jax.experimental.pallas import tpu as pltpu
from jax.sharding import PartitionSpec as P

D = 6144
QUERY_HEADS = 48
KEY_VALUE_HEADS = 8
HEAD_SIZE = 128


NEG_FILL = -1e30
EPSILON = 1e-05


def token_slots(expert_ids, slot_ids, capacity):
    in_window = jnp.logical_and(expert_ids == 0, slot_ids >= 0)
    picked = jnp.max(jnp.where(in_window, slot_ids, -1), axis=1)
    return jnp.where(picked >= 0, picked, capacity)


def other_experts(expert_ids, slot_of_token, capacity):
    partner = jnp.sum(expert_ids, axis=1)
    return jnp.zeros((capacity,), jnp.int32).at[slot_of_token].set(partner, mode="drop")


def expert_hidden(gate_sum, up_sum, square_sum, logit_sum, slot_other, model_width):
    inverse_rms = lax.rsqrt(square_sum / model_width + EPSILON)
    gate_value = gate_sum * inverse_rms[:, None]
    up_value = up_sum * inverse_rms[:, None]
    logit_value = logit_sum * inverse_rms[:, None]
    columns = jnp.arange(logit_value.shape[1], dtype=jnp.int32)
    partner_logit = jnp.sum(
        jnp.where(columns[None, :] == slot_other[:, None], logit_value, 0.0), axis=1
    )
    mixing = jax.nn.sigmoid(logit_value[:, 0] - partner_logit)
    return (jax.nn.silu(gate_value) * up_value * mixing[:, None]).astype(jnp.bfloat16)


def attention_kernel(offset_ref, q_ref, k_ref, v_ref, o_ref, *, per_shared, block_q, scale):
    seq = k_ref.shape[0]
    first = offset_ref[0] + pl.program_id(1) * block_q
    rows = first + lax.broadcasted_iota(jnp.int32, (block_q, seq), 0)
    cols = lax.broadcasted_iota(jnp.int32, (block_q, seq), 1)
    allowed = cols <= rows
    keys = k_ref[...]
    values = v_ref[...]
    for head in range(per_shared):
        query = q_ref[:, head * HEAD_SIZE : (head + 1) * HEAD_SIZE]
        scores = lax.dot_general(
            query, keys, (((1,), (1,)), ((), ())), preferred_element_type=jnp.float32
        )
        masked = jnp.where(allowed, scores, NEG_FILL)
        row_max = jnp.max(masked, axis=1, keepdims=True)
        weights = jnp.exp((masked - row_max) * scale)
        total = jnp.sum(weights, axis=1, keepdims=True)
        acc = jnp.dot(weights.astype(jnp.bfloat16), values, preferred_element_type=jnp.float32)
        o_ref[:, head * HEAD_SIZE : (head + 1) * HEAD_SIZE] = (acc / total).astype(o_ref.dtype)


def attend(queries, packed_kv, offset, shared_heads, per_shared, interpret=False):
    rows_local = queries.shape[0]
    seq = packed_kv.shape[0]
    block_q = 256 if seq <= 2048 else 128
    block_q = min(block_q, rows_local)
    width = per_shared * HEAD_SIZE
    kernel = functools.partial(
        attention_kernel,
        per_shared=per_shared,
        block_q=block_q,
        scale=1.0 / math.sqrt(HEAD_SIZE),
    )
    grid_spec = pltpu.PrefetchScalarGridSpec(
        num_scalar_prefetch=1,
        grid=(shared_heads, rows_local // block_q),
        in_specs=[
            pl.BlockSpec((block_q, width), lambda g, b, off: (b, g)),
            pl.BlockSpec((seq, HEAD_SIZE), lambda g, b, off: (0, g)),
            pl.BlockSpec((seq, HEAD_SIZE), lambda g, b, off: (0, shared_heads + g)),
        ],
        out_specs=pl.BlockSpec((block_q, width), lambda g, b, off: (b, g)),
    )
    return pl.pallas_call(
        kernel,
        grid_spec=grid_spec,
        out_shape=jax.ShapeDtypeStruct((rows_local, shared_heads * width), jnp.bfloat16),
        compiler_params=pltpu.CompilerParams(vmem_limit_bytes=48 * 1024 * 1024),
        interpret=interpret,
    )(offset, queries, packed_kv, packed_kv)


def pair_exchange(x, axis, count, bit):
    return lax.ppermute(x, axis, perm=[(i, i ^ bit) for i in range(count)])


def gather_rows(x, axis):
    count = lax.axis_size(axis)
    if count & (count - 1):
        return lax.all_gather(x, axis, axis=0, tiled=True)
    index = lax.axis_index(axis)
    out = x
    bit = 1
    while bit < count:
        other = pair_exchange(out, axis, count, bit)
        upper = (index // bit) % 2
        size = out.shape[0]
        both = jnp.zeros((2 * size,) + out.shape[1:], out.dtype)
        both = lax.dynamic_update_slice_in_dim(both, out, upper * size, 0)
        out = lax.dynamic_update_slice_in_dim(both, other, (1 - upper) * size, 0)
        bit *= 2
    return out


def gather_causal(x, axis):
    count = lax.axis_size(axis)
    if count != 4:
        return gather_rows(x, axis)
    index = lax.axis_index(axis)
    rows = x.shape[0]
    lower = lax.ppermute(x, axis, perm=[(0, 2), (1, 3)])
    pair = jnp.concatenate([x, lower], axis=0)
    other = pair_exchange(pair, axis, count, 1)
    partner = index ^ 1
    out = jnp.zeros((count * rows,) + x.shape[1:], x.dtype)
    for block, at in (
        (x, index),
        (lower, (index + 2) % 4),
        (other[:rows], partner),
        (other[rows:], (partner + 2) % 4),
    ):
        out = lax.dynamic_update_slice_in_dim(out, block, at * rows, 0)
    return out


def sum_rows(x, axis):
    count = lax.axis_size(axis)
    if count & (count - 1) or x.shape[0] % count:
        return lax.psum(x.astype(jnp.bfloat16), axis)
    index = lax.axis_index(axis)
    acc = x.astype(jnp.float32)
    bit = 1
    while bit < count // 2:
        half = acc.shape[0] // 2
        upper = (index // bit) % 2
        keep = lax.dynamic_slice_in_dim(acc, upper * half, half, 0)
        send = lax.dynamic_slice_in_dim(acc, (1 - upper) * half, half, 0)
        other = pair_exchange(send.astype(jnp.bfloat16), axis, count, bit)
        acc = keep + other.astype(jnp.float32)
        bit *= 2
    if bit < count:
        mine = acc.astype(jnp.bfloat16)
        other = pair_exchange(mine, axis, count, bit)
        upper = (index // bit) % 2
        low = jnp.where(upper == 0, mine, other).astype(jnp.float32)
        high = jnp.where(upper == 0, other, mine).astype(jnp.float32)
        acc = low + high
    out = acc.astype(jnp.bfloat16)
    bit = count // 4
    while bit >= 1:
        other = pair_exchange(out, axis, count, bit)
        upper = (index // bit) % 2
        size = out.shape[0]
        both = jnp.zeros((2 * size,) + out.shape[1:], out.dtype)
        both = lax.dynamic_update_slice_in_dim(both, out, upper * size, 0)
        out = lax.dynamic_update_slice_in_dim(both, other, (1 - upper) * size, 0)
        bit //= 2
    return out


def local(
    queries,
    key_rows,
    value_head_rows,
    residual,
    out_weight,
    norm_gain,
    router_weight,
    gate_weight,
    up_weight,
    down_weight,
    expert_ids,
    slot_ids,
):
    ctx_count = lax.axis_size("ctx")
    wide_index = lax.axis_index("wide")
    ctx_index = lax.axis_index("ctx")
    rows_local = queries.shape[0]
    heads_local = queries.shape[1] // HEAD_SIZE
    query_group_width = QUERY_HEADS // KEY_VALUE_HEADS
    shared_heads = max(1, heads_local // query_group_width)
    per_shared = heads_local // shared_heads
    first_shared = wide_index * heads_local // query_group_width
    key_used = lax.dynamic_slice_in_dim(
        key_rows, first_shared * HEAD_SIZE, shared_heads * HEAD_SIZE, 1
    )
    value_used = lax.dynamic_slice_in_dim(
        value_head_rows, first_shared * HEAD_SIZE, shared_heads * HEAD_SIZE, 1
    )
    packed_kv = gather_causal(jnp.concatenate([key_used, value_used], axis=1), "ctx")
    offset = jnp.reshape(ctx_index * rows_local, (1,)).astype(jnp.int32)
    attended = attend(queries, packed_kv, offset, shared_heads, per_shared)
    partial_out = jnp.dot(attended, out_weight, preferred_element_type=jnp.float32)
    head_sum = lax.psum_scatter(
        partial_out.astype(jnp.bfloat16), "wide", scatter_dimension=1, tiled=True
    ).astype(jnp.float32)
    resid = (residual.astype(jnp.float32) + head_sum).astype(jnp.bfloat16)
    seq_len = rows_local * ctx_count
    capacity = seq_len * 5 // 16
    width_local = resid.shape[1]
    wide_count = lax.axis_size("wide")
    chunk = capacity // wide_count
    slot_of_token = token_slots(expert_ids, slot_ids, capacity)
    partner = jnp.sum(expert_ids, axis=1)
    slot_local = lax.dynamic_slice_in_dim(slot_of_token, ctx_index * rows_local, rows_local)
    slot_ids_all = jnp.arange(capacity, dtype=jnp.int32)
    place = (slot_ids_all[:, None] == slot_local[None, :]).astype(jnp.bfloat16)
    own_rows = jnp.dot(place, resid, preferred_element_type=jnp.float32)
    buffer = sum_rows(own_rows, "ctx")
    buffer_wide = buffer.astype(jnp.float32)
    square_part = jnp.sum(buffer_wide * buffer_wide, axis=1)
    scaled = (buffer_wide * norm_gain.astype(jnp.float32)[None, :]).astype(jnp.bfloat16)
    both_part = jnp.dot(
        scaled,
        jnp.concatenate([gate_weight, up_weight], axis=1),
        preferred_element_type=jnp.float32,
    )
    logit_part = jnp.dot(scaled, router_weight, preferred_element_type=jnp.float32)
    hidden_local = gate_weight.shape[1]
    experts = logit_part.shape[1]
    pad = 128 - (experts + 1) % 128
    small = jnp.concatenate(
        [logit_part, square_part[:, None], jnp.zeros((capacity, pad), jnp.float32)], axis=1
    )
    both_sum = lax.psum_scatter(
        both_part.astype(jnp.bfloat16), "wide", scatter_dimension=0, tiled=True
    ).astype(jnp.float32)
    small_sum = lax.dynamic_slice_in_dim(
        sum_rows(small, "wide"), wide_index * chunk, chunk, 0
    ).astype(jnp.float32)
    gate_sum = both_sum[:, :hidden_local]
    up_sum = both_sum[:, hidden_local:]
    logit_sum = small_sum[:, :experts]
    square_sum = small_sum[:, experts]
    chunk_slots = wide_index * chunk + jnp.arange(chunk, dtype=jnp.int32)
    other_chunk = jnp.sum(
        jnp.where(chunk_slots[:, None] == slot_of_token[None, :], partner[None, :], 0), axis=1
    )
    hidden_chunk = expert_hidden(gate_sum, up_sum, square_sum, logit_sum, other_chunk, D)
    hidden = lax.all_gather(hidden_chunk, "wide", axis=0, tiled=True)
    expert_part = jnp.dot(hidden, down_weight, preferred_element_type=jnp.float32)
    expert_sum = sum_rows(expert_part, "ctx")
    pick = (slot_local[:, None] == slot_ids_all[None, :]).astype(jnp.bfloat16)
    moe_rows = jnp.dot(pick, expert_sum, preferred_element_type=jnp.float32)
    return (resid.astype(jnp.float32) + moe_rows).astype(jnp.bfloat16)


def solution(mesh):
    placed = (
        P(("groups", "ctx"), "wide"),
        P(("groups", "ctx"), None),
        P(("groups", "ctx"), None),
        P(("groups", "ctx"), "wide"),
        P("wide", None),
        P("wide"),
        P("wide", None),
        P("wide", "ctx"),
        P("wide", "ctx"),
        P("ctx", "wide"),
        P("groups", None),
        P("groups", None),
    )
    return jax.shard_map(
        local, mesh=mesh, in_specs=placed, out_specs=P(("groups", "ctx"), "wide"), check_vma=False
    )
```

```python
import functools
import math

import jax
import jax.numpy as jnp
from jax import lax
from jax.experimental import pallas as pl
from jax.experimental.pallas import tpu as pltpu
from jax.sharding import PartitionSpec as P

D = 6144
QUERY_HEADS = 48
KEY_VALUE_HEADS = 8
HEAD_SIZE = 128


NEG_FILL = -1e30
EPSILON = 1e-05


def token_slots(expert_ids, slot_ids, capacity):
    in_window = jnp.logical_and(expert_ids == 0, slot_ids >= 0)
    picked = jnp.max(jnp.where(in_window, slot_ids, -1), axis=1)
    return jnp.where(picked >= 0, picked, capacity)


def other_experts(expert_ids, slot_of_token, capacity):
    partner = jnp.sum(expert_ids, axis=1)
    return jnp.zeros((capacity,), jnp.int32).at[slot_of_token].set(partner, mode="drop")


def expert_hidden(gate_sum, up_sum, square_sum, logit_sum, slot_other, model_width):
    inverse_rms = lax.rsqrt(square_sum / model_width + EPSILON)
    gate_value = gate_sum * inverse_rms[:, None]
    up_value = up_sum * inverse_rms[:, None]
    logit_value = logit_sum * inverse_rms[:, None]
    columns = jnp.arange(logit_value.shape[1], dtype=jnp.int32)
    partner_logit = jnp.sum(
        jnp.where(columns[None, :] == slot_other[:, None], logit_value, 0.0), axis=1
    )
    mixing = jax.nn.sigmoid(logit_value[:, 0] - partner_logit)
    return (jax.nn.silu(gate_value) * up_value * mixing[:, None]).astype(jnp.bfloat16)


def attention_kernel(offset_ref, q_ref, k_ref, v_ref, o_ref, *, per_shared, block_q, scale):
    seq = k_ref.shape[0]
    first = offset_ref[0] + pl.program_id(1) * block_q
    rows = first + lax.broadcasted_iota(jnp.int32, (block_q, seq), 0)
    cols = lax.broadcasted_iota(jnp.int32, (block_q, seq), 1)
    allowed = cols <= rows
    keys = k_ref[...]
    values = v_ref[...]
    for head in range(per_shared):
        query = q_ref[:, head * HEAD_SIZE : (head + 1) * HEAD_SIZE]
        scores = (
            lax.dot_general(
                query, keys, (((1,), (1,)), ((), ())), preferred_element_type=jnp.float32
            )
            * scale
        )
        masked = jnp.where(allowed, scores, NEG_FILL)
        row_max = jnp.max(masked, axis=1, keepdims=True)
        weights = jnp.exp(masked - row_max)
        total = jnp.sum(weights, axis=1, keepdims=True)
        acc = jnp.dot(weights.astype(jnp.bfloat16), values, preferred_element_type=jnp.float32)
        o_ref[:, head * HEAD_SIZE : (head + 1) * HEAD_SIZE] = (acc / total).astype(o_ref.dtype)


def attend(queries, packed_kv, offset, shared_heads, per_shared, interpret=False):
    rows_local = queries.shape[0]
    seq = packed_kv.shape[0]
    block_q = 256 if seq <= 2048 else 128
    block_q = min(block_q, rows_local)
    width = per_shared * HEAD_SIZE
    kernel = functools.partial(
        attention_kernel,
        per_shared=per_shared,
        block_q=block_q,
        scale=1.0 / math.sqrt(HEAD_SIZE),
    )
    grid_spec = pltpu.PrefetchScalarGridSpec(
        num_scalar_prefetch=1,
        grid=(shared_heads, rows_local // block_q),
        in_specs=[
            pl.BlockSpec((block_q, width), lambda g, b, off: (b, g)),
            pl.BlockSpec((seq, HEAD_SIZE), lambda g, b, off: (0, g)),
            pl.BlockSpec((seq, HEAD_SIZE), lambda g, b, off: (0, shared_heads + g)),
        ],
        out_specs=pl.BlockSpec((block_q, width), lambda g, b, off: (b, g)),
    )
    return pl.pallas_call(
        kernel,
        grid_spec=grid_spec,
        out_shape=jax.ShapeDtypeStruct((rows_local, shared_heads * width), jnp.bfloat16),
        compiler_params=pltpu.CompilerParams(vmem_limit_bytes=48 * 1024 * 1024),
        interpret=interpret,
    )(offset, queries, packed_kv, packed_kv)


def pair_exchange(x, axis, count, bit):
    return lax.ppermute(x, axis, perm=[(i, i ^ bit) for i in range(count)])


def gather_rows(x, axis):
    count = lax.axis_size(axis)
    if count & (count - 1):
        return lax.all_gather(x, axis, axis=0, tiled=True)
    index = lax.axis_index(axis)
    out = x
    bit = 1
    while bit < count:
        other = pair_exchange(out, axis, count, bit)
        upper = (index // bit) % 2
        size = out.shape[0]
        both = jnp.zeros((2 * size,) + out.shape[1:], out.dtype)
        both = lax.dynamic_update_slice_in_dim(both, out, upper * size, 0)
        out = lax.dynamic_update_slice_in_dim(both, other, (1 - upper) * size, 0)
        bit *= 2
    return out


def gather_causal(x, axis):
    count = lax.axis_size(axis)
    if count != 4:
        return gather_rows(x, axis)
    index = lax.axis_index(axis)
    rows = x.shape[0]
    lower = lax.ppermute(x, axis, perm=[(0, 2), (1, 3)])
    pair = jnp.concatenate([x, lower], axis=0)
    other = pair_exchange(pair, axis, count, 1)
    partner = index ^ 1
    out = jnp.zeros((count * rows,) + x.shape[1:], x.dtype)
    for block, at in (
        (x, index),
        (lower, (index + 2) % 4),
        (other[:rows], partner),
        (other[rows:], (partner + 2) % 4),
    ):
        out = lax.dynamic_update_slice_in_dim(out, block, at * rows, 0)
    return out


def sum_rows(x, axis):
    count = lax.axis_size(axis)
    if count & (count - 1) or x.shape[0] % count:
        return lax.psum(x.astype(jnp.bfloat16), axis)
    index = lax.axis_index(axis)
    acc = x.astype(jnp.float32)
    bit = 1
    while bit < count // 2:
        half = acc.shape[0] // 2
        upper = (index // bit) % 2
        keep = lax.dynamic_slice_in_dim(acc, upper * half, half, 0)
        send = lax.dynamic_slice_in_dim(acc, (1 - upper) * half, half, 0)
        other = pair_exchange(send.astype(jnp.bfloat16), axis, count, bit)
        acc = keep + other.astype(jnp.float32)
        bit *= 2
    if bit < count:
        mine = acc.astype(jnp.bfloat16)
        other = pair_exchange(mine, axis, count, bit)
        upper = (index // bit) % 2
        low = jnp.where(upper == 0, mine, other).astype(jnp.float32)
        high = jnp.where(upper == 0, other, mine).astype(jnp.float32)
        acc = low + high
    out = acc.astype(jnp.bfloat16)
    bit = count // 4
    while bit >= 1:
        other = pair_exchange(out, axis, count, bit)
        upper = (index // bit) % 2
        size = out.shape[0]
        both = jnp.zeros((2 * size,) + out.shape[1:], out.dtype)
        both = lax.dynamic_update_slice_in_dim(both, out, upper * size, 0)
        out = lax.dynamic_update_slice_in_dim(both, other, (1 - upper) * size, 0)
        bit //= 2
    return out


def local(
    queries,
    key_rows,
    value_head_rows,
    residual,
    out_weight,
    norm_gain,
    router_weight,
    gate_weight,
    up_weight,
    down_weight,
    expert_ids,
    slot_ids,
):
    ctx_count = lax.axis_size("ctx")
    wide_index = lax.axis_index("wide")
    ctx_index = lax.axis_index("ctx")
    rows_local = queries.shape[0]
    heads_local = queries.shape[1] // HEAD_SIZE
    query_group_width = QUERY_HEADS // KEY_VALUE_HEADS
    shared_heads = max(1, heads_local // query_group_width)
    per_shared = heads_local // shared_heads
    first_shared = wide_index * heads_local // query_group_width
    key_used = lax.dynamic_slice_in_dim(
        key_rows, first_shared * HEAD_SIZE, shared_heads * HEAD_SIZE, 1
    )
    value_used = lax.dynamic_slice_in_dim(
        value_head_rows, first_shared * HEAD_SIZE, shared_heads * HEAD_SIZE, 1
    )
    packed_kv = gather_causal(jnp.concatenate([key_used, value_used], axis=1), "ctx")
    offset = jnp.reshape(ctx_index * rows_local, (1,)).astype(jnp.int32)
    attended = attend(queries, packed_kv, offset, shared_heads, per_shared)
    partial_out = jnp.dot(attended, out_weight, preferred_element_type=jnp.float32)
    head_sum = lax.psum_scatter(
        partial_out.astype(jnp.bfloat16), "wide", scatter_dimension=1, tiled=True
    ).astype(jnp.float32)
    resid = (residual.astype(jnp.float32) + head_sum).astype(jnp.bfloat16)
    seq_len = rows_local * ctx_count
    capacity = seq_len * 5 // 16
    width_local = resid.shape[1]
    wide_count = lax.axis_size("wide")
    chunk = capacity // wide_count
    slot_of_token = token_slots(expert_ids, slot_ids, capacity)
    partner = jnp.sum(expert_ids, axis=1)
    slot_local = lax.dynamic_slice_in_dim(slot_of_token, ctx_index * rows_local, rows_local)
    slot_ids_all = jnp.arange(capacity, dtype=jnp.int32)
    place = (slot_ids_all[:, None] == slot_local[None, :]).astype(jnp.bfloat16)
    own_rows = jnp.dot(place, resid, preferred_element_type=jnp.float32)
    buffer = sum_rows(own_rows, "ctx")
    buffer_wide = buffer.astype(jnp.float32)
    square_part = jnp.sum(buffer_wide * buffer_wide, axis=1)
    scaled = (buffer_wide * norm_gain.astype(jnp.float32)[None, :]).astype(jnp.bfloat16)
    both_part = jnp.dot(
        scaled,
        jnp.concatenate([gate_weight, up_weight], axis=1),
        preferred_element_type=jnp.float32,
    )
    logit_part = jnp.dot(scaled, router_weight, preferred_element_type=jnp.float32)
    hidden_local = gate_weight.shape[1]
    experts = logit_part.shape[1]
    pad = 128 - (experts + 1) % 128
    small = jnp.concatenate(
        [logit_part, square_part[:, None], jnp.zeros((capacity, pad), jnp.float32)], axis=1
    )
    both_sum = lax.psum_scatter(
        both_part.astype(jnp.bfloat16), "wide", scatter_dimension=0, tiled=True
    ).astype(jnp.float32)
    small_sum = lax.dynamic_slice_in_dim(
        sum_rows(small, "wide"), wide_index * chunk, chunk, 0
    ).astype(jnp.float32)
    gate_sum = both_sum[:, :hidden_local]
    up_sum = both_sum[:, hidden_local:]
    logit_sum = small_sum[:, :experts]
    square_sum = small_sum[:, experts]
    chunk_slots = wide_index * chunk + jnp.arange(chunk, dtype=jnp.int32)
    other_chunk = jnp.sum(
        jnp.where(chunk_slots[:, None] == slot_of_token[None, :], partner[None, :], 0), axis=1
    )
    hidden_chunk = expert_hidden(gate_sum, up_sum, square_sum, logit_sum, other_chunk, D)
    if wide_count > 4:
        hidden = lax.all_gather(hidden_chunk, "wide", axis=0, tiled=True)
        expert_part = jnp.dot(hidden, down_weight, preferred_element_type=jnp.float32)
        expert_sum = sum_rows(expert_part, "ctx")
        pick = (slot_local[:, None] == slot_ids_all[None, :]).astype(jnp.bfloat16)
        moe_rows = jnp.dot(pick, expert_sum, preferred_element_type=jnp.float32)
        return (resid.astype(jnp.float32) + moe_rows).astype(jnp.bfloat16)
    moe_rows = jnp.zeros((rows_local, width_local), jnp.float32)

    def settle(moe_rows, hidden_rows, owners):
        expert_part = jnp.dot(hidden_rows, down_weight, preferred_element_type=jnp.float32)
        expert_sum = sum_rows(expert_part, "ctx")
        for place_at, owner in enumerate(owners):
            ids = owner * chunk + jnp.arange(chunk, dtype=jnp.int32)
            valid = jnp.logical_and(owner >= 0, owner < wide_count)
            pick = jnp.logical_and(slot_local[:, None] == ids[None, :], valid)
            block = expert_sum[place_at * chunk : (place_at + 1) * chunk]
            moe_rows = moe_rows + jnp.dot(
                pick.astype(jnp.bfloat16), block, preferred_element_type=jnp.float32
            )
        return moe_rows

    moe_rows = settle(moe_rows, hidden_chunk, (wide_index,))
    rightward = [(i, i + 1) for i in range(wide_count - 1)]
    leftward = [(i + 1, i) for i in range(wide_count - 1)]
    from_left = hidden_chunk
    from_right = hidden_chunk
    for step in range(1, wide_count):
        from_left = lax.ppermute(from_left, "wide", perm=rightward)
        from_right = lax.ppermute(from_right, "wide", perm=leftward)
        moe_rows = settle(
            moe_rows,
            jnp.concatenate([from_left, from_right], axis=0),
            (wide_index - step, wide_index + step),
        )
    return (resid.astype(jnp.float32) + moe_rows).astype(jnp.bfloat16)


def solution(mesh):
    placed = (
        P(("groups", "ctx"), "wide"),
        P(("groups", "ctx"), None),
        P(("groups", "ctx"), None),
        P(("groups", "ctx"), "wide"),
        P("wide", None),
        P("wide"),
        P("wide", None),
        P("wide", "ctx"),
        P("wide", "ctx"),
        P("ctx", "wide"),
        P("groups", None),
        P("groups", None),
    )
    return jax.shard_map(
        local, mesh=mesh, in_specs=placed, out_specs=P(("groups", "ctx"), "wide"), check_vma=False
    )
```

```python
import functools
import math

import jax
import jax.numpy as jnp
from jax import lax
from jax.experimental import pallas as pl
from jax.experimental.pallas import tpu as pltpu
from jax.sharding import PartitionSpec as P

D = 6144
QUERY_HEADS = 48
KEY_VALUE_HEADS = 8
HEAD_SIZE = 128


NEG_FILL = -1e30
EPSILON = 1e-05


def token_slots(expert_ids, slot_ids, capacity):
    in_window = jnp.logical_and(expert_ids == 0, slot_ids >= 0)
    picked = jnp.max(jnp.where(in_window, slot_ids, -1), axis=1)
    return jnp.where(picked >= 0, picked, capacity)


def other_experts(expert_ids, slot_of_token, capacity):
    partner = jnp.sum(expert_ids, axis=1)
    return jnp.zeros((capacity,), jnp.int32).at[slot_of_token].set(partner, mode="drop")


def expert_hidden(gate_sum, up_sum, square_sum, logit_sum, slot_other, model_width):
    inverse_rms = lax.rsqrt(square_sum / model_width + EPSILON)
    gate_value = gate_sum * inverse_rms[:, None]
    up_value = up_sum * inverse_rms[:, None]
    logit_value = logit_sum * inverse_rms[:, None]
    columns = jnp.arange(logit_value.shape[1], dtype=jnp.int32)
    partner_logit = jnp.sum(
        jnp.where(columns[None, :] == slot_other[:, None], logit_value, 0.0), axis=1
    )
    mixing = jax.nn.sigmoid(logit_value[:, 0] - partner_logit)
    return (jax.nn.silu(gate_value) * up_value * mixing[:, None]).astype(jnp.bfloat16)


def attention_kernel(offset_ref, q_ref, k_ref, v_ref, o_ref, *, per_shared, block_q, scale):
    seq = k_ref.shape[0]
    first = offset_ref[0] + pl.program_id(1) * block_q
    rows = first + lax.broadcasted_iota(jnp.int32, (block_q, seq), 0)
    cols = lax.broadcasted_iota(jnp.int32, (block_q, seq), 1)
    allowed = cols <= rows
    keys = k_ref[...]
    values = v_ref[...]
    for head in range(per_shared):
        query = q_ref[:, head * HEAD_SIZE : (head + 1) * HEAD_SIZE]
        scores = (
            lax.dot_general(
                query, keys, (((1,), (1,)), ((), ())), preferred_element_type=jnp.float32
            )
            * scale
        )
        masked = jnp.where(allowed, scores, NEG_FILL)
        row_max = jnp.max(masked, axis=1, keepdims=True)
        weights = jnp.exp(masked - row_max)
        total = jnp.sum(weights, axis=1, keepdims=True)
        acc = jnp.dot(weights.astype(jnp.bfloat16), values, preferred_element_type=jnp.float32)
        o_ref[:, head * HEAD_SIZE : (head + 1) * HEAD_SIZE] = (acc / total).astype(o_ref.dtype)


def attend(queries, packed_kv, offset, shared_heads, per_shared, interpret=False):
    rows_local = queries.shape[0]
    seq = packed_kv.shape[0]
    block_q = 256 if seq <= 2048 else 128
    block_q = min(block_q, rows_local)
    width = per_shared * HEAD_SIZE
    kernel = functools.partial(
        attention_kernel,
        per_shared=per_shared,
        block_q=block_q,
        scale=1.0 / math.sqrt(HEAD_SIZE),
    )
    grid_spec = pltpu.PrefetchScalarGridSpec(
        num_scalar_prefetch=1,
        grid=(shared_heads, rows_local // block_q),
        in_specs=[
            pl.BlockSpec((block_q, width), lambda g, b, off: (b, g)),
            pl.BlockSpec((seq, HEAD_SIZE), lambda g, b, off: (0, g)),
            pl.BlockSpec((seq, HEAD_SIZE), lambda g, b, off: (0, shared_heads + g)),
        ],
        out_specs=pl.BlockSpec((block_q, width), lambda g, b, off: (b, g)),
    )
    return pl.pallas_call(
        kernel,
        grid_spec=grid_spec,
        out_shape=jax.ShapeDtypeStruct((rows_local, shared_heads * width), jnp.bfloat16),
        compiler_params=pltpu.CompilerParams(vmem_limit_bytes=48 * 1024 * 1024),
        interpret=interpret,
    )(offset, queries, packed_kv, packed_kv)


def pair_exchange(x, axis, count, bit):
    return lax.ppermute(x, axis, perm=[(i, i ^ bit) for i in range(count)])


def gather_rows(x, axis):
    count = lax.axis_size(axis)
    if count & (count - 1):
        return lax.all_gather(x, axis, axis=0, tiled=True)
    index = lax.axis_index(axis)
    out = x
    bit = 1
    while bit < count:
        other = pair_exchange(out, axis, count, bit)
        upper = (index // bit) % 2
        size = out.shape[0]
        both = jnp.zeros((2 * size,) + out.shape[1:], out.dtype)
        both = lax.dynamic_update_slice_in_dim(both, out, upper * size, 0)
        out = lax.dynamic_update_slice_in_dim(both, other, (1 - upper) * size, 0)
        bit *= 2
    return out


def gather_causal(x, axis):
    count = lax.axis_size(axis)
    if count != 4:
        return gather_rows(x, axis)
    index = lax.axis_index(axis)
    rows = x.shape[0]
    lower = lax.ppermute(x, axis, perm=[(0, 2), (1, 3)])
    pair = jnp.concatenate([x, lower], axis=0)
    other = pair_exchange(pair, axis, count, 1)
    partner = index ^ 1
    out = jnp.zeros((count * rows,) + x.shape[1:], x.dtype)
    for block, at in (
        (x, index),
        (lower, (index + 2) % 4),
        (other[:rows], partner),
        (other[rows:], (partner + 2) % 4),
    ):
        out = lax.dynamic_update_slice_in_dim(out, block, at * rows, 0)
    return out


def sum_rows(x, axis):
    count = lax.axis_size(axis)
    if count & (count - 1) or x.shape[0] % count:
        return lax.psum(x.astype(jnp.bfloat16), axis)
    index = lax.axis_index(axis)
    acc = x.astype(jnp.float32)
    bit = 1
    while bit < count // 2:
        half = acc.shape[0] // 2
        upper = (index // bit) % 2
        keep = lax.dynamic_slice_in_dim(acc, upper * half, half, 0)
        send = lax.dynamic_slice_in_dim(acc, (1 - upper) * half, half, 0)
        other = pair_exchange(send.astype(jnp.bfloat16), axis, count, bit)
        acc = keep + other.astype(jnp.float32)
        bit *= 2
    if bit < count:
        mine = acc.astype(jnp.bfloat16)
        other = pair_exchange(mine, axis, count, bit)
        upper = (index // bit) % 2
        low = jnp.where(upper == 0, mine, other).astype(jnp.float32)
        high = jnp.where(upper == 0, other, mine).astype(jnp.float32)
        acc = low + high
    out = acc.astype(jnp.bfloat16)
    bit = count // 4
    while bit >= 1:
        other = pair_exchange(out, axis, count, bit)
        upper = (index // bit) % 2
        size = out.shape[0]
        both = jnp.zeros((2 * size,) + out.shape[1:], out.dtype)
        both = lax.dynamic_update_slice_in_dim(both, out, upper * size, 0)
        out = lax.dynamic_update_slice_in_dim(both, other, (1 - upper) * size, 0)
        bit //= 2
    return out


def local(
    queries,
    key_rows,
    value_head_rows,
    residual,
    out_weight,
    norm_gain,
    router_weight,
    gate_weight,
    up_weight,
    down_weight,
    expert_ids,
    slot_ids,
):
    ctx_count = lax.axis_size("ctx")
    wide_index = lax.axis_index("wide")
    ctx_index = lax.axis_index("ctx")
    rows_local = queries.shape[0]
    heads_local = queries.shape[1] // HEAD_SIZE
    query_group_width = QUERY_HEADS // KEY_VALUE_HEADS
    shared_heads = max(1, heads_local // query_group_width)
    per_shared = heads_local // shared_heads
    first_shared = wide_index * heads_local // query_group_width
    key_used = lax.dynamic_slice_in_dim(
        key_rows, first_shared * HEAD_SIZE, shared_heads * HEAD_SIZE, 1
    )
    value_used = lax.dynamic_slice_in_dim(
        value_head_rows, first_shared * HEAD_SIZE, shared_heads * HEAD_SIZE, 1
    )
    packed_kv = gather_causal(jnp.concatenate([key_used, value_used], axis=1), "ctx")
    offset = jnp.reshape(ctx_index * rows_local, (1,)).astype(jnp.int32)
    attended = attend(queries, packed_kv, offset, shared_heads, per_shared)
    partial_out = jnp.dot(attended, out_weight, preferred_element_type=jnp.float32)
    head_sum = lax.psum_scatter(
        partial_out.astype(jnp.bfloat16), "wide", scatter_dimension=1, tiled=True
    ).astype(jnp.float32)
    resid = (residual.astype(jnp.float32) + head_sum).astype(jnp.bfloat16)
    seq_len = rows_local * ctx_count
    capacity = seq_len * 5 // 16
    width_local = resid.shape[1]
    wide_count = lax.axis_size("wide")
    chunk = capacity // wide_count
    slot_of_token = token_slots(expert_ids, slot_ids, capacity)
    partner = jnp.sum(expert_ids, axis=1)
    slot_local = lax.dynamic_slice_in_dim(slot_of_token, ctx_index * rows_local, rows_local)
    slot_ids_all = jnp.arange(capacity, dtype=jnp.int32)
    place = (slot_ids_all[:, None] == slot_local[None, :]).astype(jnp.bfloat16)
    own_rows = jnp.dot(place, resid, preferred_element_type=jnp.float32)
    buffer = sum_rows(own_rows, "ctx")
    buffer_wide = buffer.astype(jnp.float32)
    square_part = jnp.sum(buffer_wide * buffer_wide, axis=1)
    scaled = (buffer_wide * norm_gain.astype(jnp.float32)[None, :]).astype(jnp.bfloat16)
    both_part = jnp.dot(
        scaled,
        jnp.concatenate([gate_weight, up_weight], axis=1),
        preferred_element_type=jnp.float32,
    )
    logit_part = jnp.dot(scaled, router_weight, preferred_element_type=jnp.float32)
    hidden_local = gate_weight.shape[1]
    experts = logit_part.shape[1]
    pad = 128 - (experts + 1) % 128
    small = jnp.concatenate(
        [logit_part, square_part[:, None], jnp.zeros((capacity, pad), jnp.float32)], axis=1
    )
    both_sum = lax.psum_scatter(
        both_part.astype(jnp.bfloat16), "wide", scatter_dimension=0, tiled=True
    ).astype(jnp.float32)
    small_sum = lax.dynamic_slice_in_dim(
        sum_rows(small, "wide"), wide_index * chunk, chunk, 0
    ).astype(jnp.float32)
    gate_sum = both_sum[:, :hidden_local]
    up_sum = both_sum[:, hidden_local:]
    logit_sum = small_sum[:, :experts]
    square_sum = small_sum[:, experts]
    chunk_slots = wide_index * chunk + jnp.arange(chunk, dtype=jnp.int32)
    other_chunk = jnp.sum(
        jnp.where(chunk_slots[:, None] == slot_of_token[None, :], partner[None, :], 0), axis=1
    )
    hidden_chunk = expert_hidden(gate_sum, up_sum, square_sum, logit_sum, other_chunk, D)
    if wide_count > 4:
        hidden = lax.all_gather(hidden_chunk, "wide", axis=0, tiled=True)
        expert_part = jnp.dot(hidden, down_weight, preferred_element_type=jnp.float32)
        expert_sum = sum_rows(expert_part, "ctx")
        pick = (slot_local[:, None] == slot_ids_all[None, :]).astype(jnp.bfloat16)
        moe_rows = jnp.dot(pick, expert_sum, preferred_element_type=jnp.float32)
        return (resid.astype(jnp.float32) + moe_rows).astype(jnp.bfloat16)
    span = 3 * wide_count - 2
    gathered = jnp.zeros((span * chunk, hidden_chunk.shape[1]), hidden_chunk.dtype)
    gathered = lax.dynamic_update_slice_in_dim(
        gathered, hidden_chunk, (wide_index + wide_count - 1) * chunk, 0
    )
    rightward = [(i, i + 1) for i in range(wide_count - 1)]
    leftward = [(i + 1, i) for i in range(wide_count - 1)]
    from_left = hidden_chunk
    from_right = hidden_chunk
    for step in range(1, wide_count):
        from_left = lax.ppermute(from_left, "wide", perm=rightward)
        from_right = lax.ppermute(from_right, "wide", perm=leftward)
        gathered = lax.dynamic_update_slice_in_dim(
            gathered, from_left, (wide_index - step + wide_count - 1) * chunk, 0
        )
        gathered = lax.dynamic_update_slice_in_dim(
            gathered, from_right, (wide_index + step + wide_count - 1) * chunk, 0
        )
    hidden = lax.slice_in_dim(
        gathered, (wide_count - 1) * chunk, (2 * wide_count - 1) * chunk, axis=0
    )
    expert_part = jnp.dot(hidden, down_weight, preferred_element_type=jnp.float32)
    expert_sum = sum_rows(expert_part, "ctx")
    pick = (slot_local[:, None] == slot_ids_all[None, :]).astype(jnp.bfloat16)
    moe_rows = jnp.dot(pick, expert_sum, preferred_element_type=jnp.float32)
    return (resid.astype(jnp.float32) + moe_rows).astype(jnp.bfloat16)


def solution(mesh):
    placed = (
        P(("groups", "ctx"), "wide"),
        P(("groups", "ctx"), None),
        P(("groups", "ctx"), None),
        P(("groups", "ctx"), "wide"),
        P("wide", None),
        P("wide"),
        P("wide", None),
        P("wide", "ctx"),
        P("wide", "ctx"),
        P("ctx", "wide"),
        P("groups", None),
        P("groups", None),
    )
    return jax.shard_map(
        local, mesh=mesh, in_specs=placed, out_specs=P(("groups", "ctx"), "wide"), check_vma=False
    )
```

```python
import functools
import math

import jax
import jax.numpy as jnp
from jax import lax
from jax.experimental import pallas as pl
from jax.experimental.pallas import tpu as pltpu
from jax.sharding import PartitionSpec as P

D = 6144
QUERY_HEADS = 48
KEY_VALUE_HEADS = 8
HEAD_SIZE = 128


NEG_FILL = -1e30
EPSILON = 1e-05


def token_slots(expert_ids, slot_ids, capacity):
    in_window = jnp.logical_and(expert_ids == 0, slot_ids >= 0)
    picked = jnp.max(jnp.where(in_window, slot_ids, -1), axis=1)
    return jnp.where(picked >= 0, picked, capacity)


def other_experts(expert_ids, slot_of_token, capacity):
    partner = jnp.sum(expert_ids, axis=1)
    return jnp.zeros((capacity,), jnp.int32).at[slot_of_token].set(partner, mode="drop")


def expert_hidden(gate_sum, up_sum, square_sum, logit_sum, slot_other, model_width):
    inverse_rms = lax.rsqrt(square_sum / model_width + EPSILON)
    gate_value = gate_sum * inverse_rms[:, None]
    up_value = up_sum * inverse_rms[:, None]
    logit_value = logit_sum * inverse_rms[:, None]
    columns = jnp.arange(logit_value.shape[1], dtype=jnp.int32)
    partner_logit = jnp.sum(
        jnp.where(columns[None, :] == slot_other[:, None], logit_value, 0.0), axis=1
    )
    mixing = jax.nn.sigmoid(logit_value[:, 0] - partner_logit)
    return (jax.nn.silu(gate_value) * up_value * mixing[:, None]).astype(jnp.bfloat16)


def attention_kernel(offset_ref, q_ref, k_ref, v_ref, o_ref, *, per_shared, block_q, scale):
    seq = k_ref.shape[0]
    first = offset_ref[0] + pl.program_id(1) * block_q
    rows = first + lax.broadcasted_iota(jnp.int32, (block_q, seq), 0)
    cols = lax.broadcasted_iota(jnp.int32, (block_q, seq), 1)
    allowed = cols <= rows
    keys = k_ref[...]
    values = v_ref[...]
    def one_head(head, carry):
        start = pl.multiple_of(head * HEAD_SIZE, HEAD_SIZE)
        query = q_ref[:, pl.ds(start, HEAD_SIZE)]
        scores = (
            lax.dot_general(
                query, keys, (((1,), (1,)), ((), ())), preferred_element_type=jnp.float32
            )
            * scale
        )
        masked = jnp.where(allowed, scores, NEG_FILL)
        row_max = jnp.max(masked, axis=1, keepdims=True)
        weights = jnp.exp(masked - row_max)
        total = jnp.sum(weights, axis=1, keepdims=True)
        acc = jnp.dot(weights.astype(jnp.bfloat16), values, preferred_element_type=jnp.float32)
        o_ref[:, pl.ds(start, HEAD_SIZE)] = (acc / total).astype(o_ref.dtype)
        return carry

    lax.fori_loop(0, per_shared, one_head, 0)


def attend(queries, packed_kv, offset, shared_heads, per_shared, interpret=False):
    rows_local = queries.shape[0]
    seq = packed_kv.shape[0]
    block_q = 512 if seq <= 2048 else 128
    block_q = min(block_q, rows_local)
    width = per_shared * HEAD_SIZE
    kernel = functools.partial(
        attention_kernel,
        per_shared=per_shared,
        block_q=block_q,
        scale=1.0 / math.sqrt(HEAD_SIZE),
    )
    grid_spec = pltpu.PrefetchScalarGridSpec(
        num_scalar_prefetch=1,
        grid=(shared_heads, rows_local // block_q),
        in_specs=[
            pl.BlockSpec((block_q, width), lambda g, b, off: (b, g)),
            pl.BlockSpec((seq, HEAD_SIZE), lambda g, b, off: (0, g)),
            pl.BlockSpec((seq, HEAD_SIZE), lambda g, b, off: (0, shared_heads + g)),
        ],
        out_specs=pl.BlockSpec((block_q, width), lambda g, b, off: (b, g)),
    )
    return pl.pallas_call(
        kernel,
        grid_spec=grid_spec,
        out_shape=jax.ShapeDtypeStruct((rows_local, shared_heads * width), jnp.bfloat16),
        compiler_params=pltpu.CompilerParams(vmem_limit_bytes=48 * 1024 * 1024),
        interpret=interpret,
    )(offset, queries, packed_kv, packed_kv)


def pair_exchange(x, axis, count, bit):
    return lax.ppermute(x, axis, perm=[(i, i ^ bit) for i in range(count)])


def gather_rows(x, axis):
    count = lax.axis_size(axis)
    if count & (count - 1):
        return lax.all_gather(x, axis, axis=0, tiled=True)
    index = lax.axis_index(axis)
    out = x
    bit = 1
    while bit < count:
        other = pair_exchange(out, axis, count, bit)
        upper = (index // bit) % 2
        size = out.shape[0]
        both = jnp.zeros((2 * size,) + out.shape[1:], out.dtype)
        both = lax.dynamic_update_slice_in_dim(both, out, upper * size, 0)
        out = lax.dynamic_update_slice_in_dim(both, other, (1 - upper) * size, 0)
        bit *= 2
    return out


def gather_causal(x, axis):
    count = lax.axis_size(axis)
    if count != 4:
        return gather_rows(x, axis)
    index = lax.axis_index(axis)
    rows = x.shape[0]
    lower = lax.ppermute(x, axis, perm=[(0, 2), (1, 3)])
    pair = jnp.concatenate([x, lower], axis=0)
    other = pair_exchange(pair, axis, count, 1)
    partner = index ^ 1
    out = jnp.zeros((count * rows,) + x.shape[1:], x.dtype)
    for block, at in (
        (x, index),
        (lower, (index + 2) % 4),
        (other[:rows], partner),
        (other[rows:], (partner + 2) % 4),
    ):
        out = lax.dynamic_update_slice_in_dim(out, block, at * rows, 0)
    return out


def sum_rows(x, axis):
    count = lax.axis_size(axis)
    if count & (count - 1) or x.shape[0] % count:
        return lax.psum(x.astype(jnp.bfloat16), axis)
    index = lax.axis_index(axis)
    acc = x.astype(jnp.float32)
    bit = 1
    while bit < count // 2:
        half = acc.shape[0] // 2
        upper = (index // bit) % 2
        keep = lax.dynamic_slice_in_dim(acc, upper * half, half, 0)
        send = lax.dynamic_slice_in_dim(acc, (1 - upper) * half, half, 0)
        other = pair_exchange(send.astype(jnp.bfloat16), axis, count, bit)
        acc = keep + other.astype(jnp.float32)
        bit *= 2
    if bit < count:
        mine = acc.astype(jnp.bfloat16)
        other = pair_exchange(mine, axis, count, bit)
        upper = (index // bit) % 2
        low = jnp.where(upper == 0, mine, other).astype(jnp.float32)
        high = jnp.where(upper == 0, other, mine).astype(jnp.float32)
        acc = low + high
    out = acc.astype(jnp.bfloat16)
    bit = count // 4
    while bit >= 1:
        other = pair_exchange(out, axis, count, bit)
        upper = (index // bit) % 2
        size = out.shape[0]
        both = jnp.zeros((2 * size,) + out.shape[1:], out.dtype)
        both = lax.dynamic_update_slice_in_dim(both, out, upper * size, 0)
        out = lax.dynamic_update_slice_in_dim(both, other, (1 - upper) * size, 0)
        bit //= 2
    return out


def local(
    queries,
    key_rows,
    value_head_rows,
    residual,
    out_weight,
    norm_gain,
    router_weight,
    gate_weight,
    up_weight,
    down_weight,
    expert_ids,
    slot_ids,
):
    ctx_count = lax.axis_size("ctx")
    wide_index = lax.axis_index("wide")
    ctx_index = lax.axis_index("ctx")
    rows_local = queries.shape[0]
    heads_local = queries.shape[1] // HEAD_SIZE
    query_group_width = QUERY_HEADS // KEY_VALUE_HEADS
    shared_heads = max(1, heads_local // query_group_width)
    per_shared = heads_local // shared_heads
    first_shared = wide_index * heads_local // query_group_width
    key_used = lax.dynamic_slice_in_dim(
        key_rows, first_shared * HEAD_SIZE, shared_heads * HEAD_SIZE, 1
    )
    value_used = lax.dynamic_slice_in_dim(
        value_head_rows, first_shared * HEAD_SIZE, shared_heads * HEAD_SIZE, 1
    )
    packed_kv = gather_causal(jnp.concatenate([key_used, value_used], axis=1), "ctx")
    offset = jnp.reshape(ctx_index * rows_local, (1,)).astype(jnp.int32)
    attended = attend(queries, packed_kv, offset, shared_heads, per_shared)
    partial_out = jnp.dot(attended, out_weight, preferred_element_type=jnp.float32)
    head_sum = lax.psum_scatter(
        partial_out.astype(jnp.bfloat16), "wide", scatter_dimension=1, tiled=True
    ).astype(jnp.float32)
    resid = (residual.astype(jnp.float32) + head_sum).astype(jnp.bfloat16)
    seq_len = rows_local * ctx_count
    capacity = seq_len * 5 // 16
    width_local = resid.shape[1]
    wide_count = lax.axis_size("wide")
    chunk = capacity // wide_count
    slot_of_token = token_slots(expert_ids, slot_ids, capacity)
    partner = jnp.sum(expert_ids, axis=1)
    slot_local = lax.dynamic_slice_in_dim(slot_of_token, ctx_index * rows_local, rows_local)
    slot_ids_all = jnp.arange(capacity, dtype=jnp.int32)
    place = (slot_ids_all[:, None] == slot_local[None, :]).astype(jnp.bfloat16)
    own_rows = jnp.dot(place, resid, preferred_element_type=jnp.float32)
    buffer = sum_rows(own_rows, "ctx")
    buffer_wide = buffer.astype(jnp.float32)
    square_part = jnp.sum(buffer_wide * buffer_wide, axis=1)
    scaled = (buffer_wide * norm_gain.astype(jnp.float32)[None, :]).astype(jnp.bfloat16)
    both_part = jnp.dot(
        scaled,
        jnp.concatenate([gate_weight, up_weight], axis=1),
        preferred_element_type=jnp.float32,
    )
    logit_part = jnp.dot(scaled, router_weight, preferred_element_type=jnp.float32)
    hidden_local = gate_weight.shape[1]
    experts = logit_part.shape[1]
    pad = 128 - (experts + 1) % 128
    small = jnp.concatenate(
        [logit_part, square_part[:, None], jnp.zeros((capacity, pad), jnp.float32)], axis=1
    )
    both_sum = lax.psum_scatter(
        both_part.astype(jnp.bfloat16), "wide", scatter_dimension=0, tiled=True
    ).astype(jnp.float32)
    small_sum = lax.dynamic_slice_in_dim(
        sum_rows(small, "wide"), wide_index * chunk, chunk, 0
    ).astype(jnp.float32)
    gate_sum = both_sum[:, :hidden_local]
    up_sum = both_sum[:, hidden_local:]
    logit_sum = small_sum[:, :experts]
    square_sum = small_sum[:, experts]
    chunk_slots = wide_index * chunk + jnp.arange(chunk, dtype=jnp.int32)
    other_chunk = jnp.sum(
        jnp.where(chunk_slots[:, None] == slot_of_token[None, :], partner[None, :], 0), axis=1
    )
    hidden_chunk = expert_hidden(gate_sum, up_sum, square_sum, logit_sum, other_chunk, D)
    hidden = lax.all_gather(hidden_chunk, "wide", axis=0, tiled=True)
    expert_part = jnp.dot(hidden, down_weight, preferred_element_type=jnp.float32)
    expert_sum = sum_rows(expert_part, "ctx")
    pick = (slot_local[:, None] == slot_ids_all[None, :]).astype(jnp.bfloat16)
    moe_rows = jnp.dot(pick, expert_sum, preferred_element_type=jnp.float32)
    return (resid.astype(jnp.float32) + moe_rows).astype(jnp.bfloat16)


def solution(mesh):
    placed = (
        P(("groups", "ctx"), "wide"),
        P(("groups", "ctx"), None),
        P(("groups", "ctx"), None),
        P(("groups", "ctx"), "wide"),
        P("wide", None),
        P("wide"),
        P("wide", None),
        P("wide", "ctx"),
        P("wide", "ctx"),
        P("ctx", "wide"),
        P("groups", None),
        P("groups", None),
    )
    return jax.shard_map(
        local, mesh=mesh, in_specs=placed, out_specs=P(("groups", "ctx"), "wide"), check_vma=False
    )
```

```python
import functools
import math

import jax
import jax.numpy as jnp
from jax import lax
from jax.experimental import pallas as pl
from jax.experimental.pallas import tpu as pltpu
from jax.sharding import PartitionSpec as P

D = 6144
QUERY_HEADS = 48
KEY_VALUE_HEADS = 8
HEAD_SIZE = 128


NEG_FILL = -1e30
EPSILON = 1e-05


def token_slots(expert_ids, slot_ids, capacity):
    in_window = jnp.logical_and(expert_ids == 0, slot_ids >= 0)
    picked = jnp.max(jnp.where(in_window, slot_ids, -1), axis=1)
    return jnp.where(picked >= 0, picked, capacity)


def other_experts(expert_ids, slot_of_token, capacity):
    partner = jnp.sum(expert_ids, axis=1)
    return jnp.zeros((capacity,), jnp.int32).at[slot_of_token].set(partner, mode="drop")


def expert_hidden(gate_sum, up_sum, square_sum, logit_sum, slot_other, model_width):
    inverse_rms = lax.rsqrt(square_sum / model_width + EPSILON)
    gate_value = gate_sum * inverse_rms[:, None]
    up_value = up_sum * inverse_rms[:, None]
    logit_value = logit_sum * inverse_rms[:, None]
    columns = jnp.arange(logit_value.shape[1], dtype=jnp.int32)
    partner_logit = jnp.sum(
        jnp.where(columns[None, :] == slot_other[:, None], logit_value, 0.0), axis=1
    )
    mixing = jax.nn.sigmoid(logit_value[:, 0] - partner_logit)
    return (jax.nn.silu(gate_value) * up_value * mixing[:, None]).astype(jnp.bfloat16)


def attention_kernel(offset_ref, q_ref, k_ref, v_ref, o_ref, *, per_shared, block_q, scale):
    seq = k_ref.shape[0]
    first = offset_ref[0] + pl.program_id(1) * block_q
    rows = first + lax.broadcasted_iota(jnp.int32, (block_q, seq), 0)
    cols = lax.broadcasted_iota(jnp.int32, (block_q, seq), 1)
    allowed = cols <= rows
    keys = k_ref[...]
    values = v_ref[...]
    for head in range(per_shared):
        query = q_ref[:, head * HEAD_SIZE : (head + 1) * HEAD_SIZE]
        scores = (
            lax.dot_general(
                query, keys, (((1,), (1,)), ((), ())), preferred_element_type=jnp.float32
            )
            * scale
        )
        masked = jnp.where(allowed, scores, NEG_FILL)
        row_max = jnp.max(masked, axis=1, keepdims=True)
        weights = jnp.exp(masked - row_max)
        total = jnp.sum(weights, axis=1, keepdims=True)
        acc = jnp.dot(weights.astype(jnp.bfloat16), values, preferred_element_type=jnp.float32)
        o_ref[:, head * HEAD_SIZE : (head + 1) * HEAD_SIZE] = (acc / total).astype(o_ref.dtype)


def attend(queries, packed_kv, offset, shared_heads, per_shared, interpret=False):
    rows_local = queries.shape[0]
    seq = packed_kv.shape[0]
    block_q = 256 if seq <= 2048 else 128
    block_q = min(block_q, rows_local)
    width = per_shared * HEAD_SIZE
    kernel = functools.partial(
        attention_kernel,
        per_shared=per_shared,
        block_q=block_q,
        scale=1.0 / math.sqrt(HEAD_SIZE),
    )
    grid_spec = pltpu.PrefetchScalarGridSpec(
        num_scalar_prefetch=1,
        grid=(shared_heads, rows_local // block_q),
        in_specs=[
            pl.BlockSpec((block_q, width), lambda g, b, off: (b, g)),
            pl.BlockSpec((seq, HEAD_SIZE), lambda g, b, off: (0, g)),
            pl.BlockSpec((seq, HEAD_SIZE), lambda g, b, off: (0, shared_heads + g)),
        ],
        out_specs=pl.BlockSpec((block_q, width), lambda g, b, off: (b, g)),
    )
    return pl.pallas_call(
        kernel,
        grid_spec=grid_spec,
        out_shape=jax.ShapeDtypeStruct((rows_local, shared_heads * width), jnp.bfloat16),
        compiler_params=pltpu.CompilerParams(vmem_limit_bytes=48 * 1024 * 1024),
        interpret=interpret,
    )(offset, queries, packed_kv, packed_kv)


def pair_exchange(x, axis, count, bit):
    return lax.ppermute(x, axis, perm=[(i, i ^ bit) for i in range(count)])


def gather_rows(x, axis):
    count = lax.axis_size(axis)
    if count & (count - 1):
        return lax.all_gather(x, axis, axis=0, tiled=True)
    index = lax.axis_index(axis)
    out = x
    bit = 1
    while bit < count:
        other = pair_exchange(out, axis, count, bit)
        upper = (index // bit) % 2
        size = out.shape[0]
        both = jnp.zeros((2 * size,) + out.shape[1:], out.dtype)
        both = lax.dynamic_update_slice_in_dim(both, out, upper * size, 0)
        out = lax.dynamic_update_slice_in_dim(both, other, (1 - upper) * size, 0)
        bit *= 2
    return out


def gather_causal(x, axis):
    count = lax.axis_size(axis)
    if count != 4:
        return gather_rows(x, axis)
    index = lax.axis_index(axis)
    rows = x.shape[0]
    lower = lax.ppermute(x, axis, perm=[(0, 2), (1, 3)])
    pair = jnp.concatenate([x, lower], axis=0)
    other = pair_exchange(pair, axis, count, 1)
    partner = index ^ 1
    out = jnp.zeros((count * rows,) + x.shape[1:], x.dtype)
    for block, at in (
        (x, index),
        (lower, (index + 2) % 4),
        (other[:rows], partner),
        (other[rows:], (partner + 2) % 4),
    ):
        out = lax.dynamic_update_slice_in_dim(out, block, at * rows, 0)
    return out


def sum_rows(x, axis):
    count = lax.axis_size(axis)
    if count & (count - 1) or x.shape[0] % count:
        return lax.psum(x.astype(jnp.bfloat16), axis)
    index = lax.axis_index(axis)
    acc = x.astype(jnp.float32)
    bit = 1
    while bit < count // 2:
        half = acc.shape[0] // 2
        upper = (index // bit) % 2
        keep = lax.dynamic_slice_in_dim(acc, upper * half, half, 0)
        send = lax.dynamic_slice_in_dim(acc, (1 - upper) * half, half, 0)
        other = pair_exchange(send.astype(jnp.bfloat16), axis, count, bit)
        acc = keep + other.astype(jnp.float32)
        bit *= 2
    if bit < count:
        mine = acc.astype(jnp.bfloat16)
        other = pair_exchange(mine, axis, count, bit)
        upper = (index // bit) % 2
        low = jnp.where(upper == 0, mine, other).astype(jnp.float32)
        high = jnp.where(upper == 0, other, mine).astype(jnp.float32)
        acc = low + high
    out = acc.astype(jnp.bfloat16)
    bit = count // 4
    while bit >= 1:
        other = pair_exchange(out, axis, count, bit)
        upper = (index // bit) % 2
        size = out.shape[0]
        both = jnp.zeros((2 * size,) + out.shape[1:], out.dtype)
        both = lax.dynamic_update_slice_in_dim(both, out, upper * size, 0)
        out = lax.dynamic_update_slice_in_dim(both, other, (1 - upper) * size, 0)
        bit //= 2
    return out


def local(
    queries,
    key_rows,
    value_head_rows,
    residual,
    out_weight,
    norm_gain,
    router_weight,
    gate_weight,
    up_weight,
    down_weight,
    expert_ids,
    slot_ids,
):
    ctx_count = lax.axis_size("ctx")
    wide_index = lax.axis_index("wide")
    ctx_index = lax.axis_index("ctx")
    rows_local = queries.shape[0]
    heads_local = queries.shape[1] // HEAD_SIZE
    query_group_width = QUERY_HEADS // KEY_VALUE_HEADS
    shared_heads = max(1, heads_local // query_group_width)
    per_shared = heads_local // shared_heads
    first_shared = wide_index * heads_local // query_group_width
    key_used = lax.dynamic_slice_in_dim(
        key_rows, first_shared * HEAD_SIZE, shared_heads * HEAD_SIZE, 1
    )
    value_used = lax.dynamic_slice_in_dim(
        value_head_rows, first_shared * HEAD_SIZE, shared_heads * HEAD_SIZE, 1
    )
    packed_kv = gather_causal(jnp.concatenate([key_used, value_used], axis=1), "ctx")
    offset = jnp.reshape(ctx_index * rows_local, (1,)).astype(jnp.int32)
    attended = attend(queries, packed_kv, offset, shared_heads, per_shared)
    partial_out = jnp.dot(attended, out_weight, preferred_element_type=jnp.float32)
    head_sum = lax.psum_scatter(
        partial_out.astype(jnp.bfloat16), "wide", scatter_dimension=1, tiled=True
    ).astype(jnp.float32)
    resid = (residual.astype(jnp.float32) + head_sum).astype(jnp.bfloat16)
    seq_len = rows_local * ctx_count
    capacity = seq_len * 5 // 16
    width_local = resid.shape[1]
    wide_count = lax.axis_size("wide")
    chunk = capacity // wide_count
    slot_of_token = token_slots(expert_ids, slot_ids, capacity)
    partner = jnp.sum(expert_ids, axis=1)
    slot_local = lax.dynamic_slice_in_dim(slot_of_token, ctx_index * rows_local, rows_local)
    slot_ids_all = jnp.arange(capacity, dtype=jnp.int32)
    place = (slot_ids_all[:, None] == slot_local[None, :]).astype(jnp.bfloat16)
    own_rows = jnp.dot(place, resid, preferred_element_type=jnp.float32)
    buffer = sum_rows(own_rows, "ctx")
    buffer_wide = buffer.astype(jnp.float32)
    square_part = jnp.sum(buffer_wide * buffer_wide, axis=1)
    scaled = (buffer_wide * norm_gain.astype(jnp.float32)[None, :]).astype(jnp.bfloat16)
    both_part = jnp.dot(
        scaled,
        jnp.concatenate([gate_weight, up_weight], axis=1),
        preferred_element_type=jnp.float32,
    )
    logit_part = jnp.dot(scaled, router_weight, preferred_element_type=jnp.float32)
    hidden_local = gate_weight.shape[1]
    experts = logit_part.shape[1]
    pad = 128 - (experts + 1) % 128
    small = jnp.concatenate(
        [logit_part, square_part[:, None], jnp.zeros((capacity, pad), jnp.float32)], axis=1
    )
    both_sum = lax.psum_scatter(
        both_part.astype(jnp.bfloat16), "wide", scatter_dimension=0, tiled=True
    ).astype(jnp.float32)
    small_sum = lax.dynamic_slice_in_dim(
        sum_rows(small, "wide"), wide_index * chunk, chunk, 0
    ).astype(jnp.float32)
    gate_sum = both_sum[:, :hidden_local]
    up_sum = both_sum[:, hidden_local:]
    logit_sum = small_sum[:, :experts]
    square_sum = small_sum[:, experts]
    chunk_slots = wide_index * chunk + jnp.arange(chunk, dtype=jnp.int32)
    other_chunk = jnp.sum(
        jnp.where(chunk_slots[:, None] == slot_of_token[None, :], partner[None, :], 0), axis=1
    )
    hidden_chunk = expert_hidden(gate_sum, up_sum, square_sum, logit_sum, other_chunk, D)
    hidden = lax.all_gather(hidden_chunk, "wide", axis=0, tiled=True)
    expert_part = jnp.dot(hidden, down_weight, preferred_element_type=jnp.float32)
    expert_sum = sum_rows(expert_part, "ctx")
    pick = (slot_local[:, None] == slot_ids_all[None, :]).astype(jnp.bfloat16)
    moe_rows = jnp.dot(pick, expert_sum, preferred_element_type=jnp.float32)
    return (resid.astype(jnp.float32) + moe_rows).astype(jnp.bfloat16)


def solution(mesh):
    placed = (
        P(("groups", "ctx"), "wide"),
        P(("groups", "ctx"), None),
        P(("groups", "ctx"), None),
        P(("groups", "ctx"), "wide"),
        P("wide", None),
        P("wide"),
        P("wide", None),
        P("wide", "ctx"),
        P("wide", "ctx"),
        P("ctx", "wide"),
        P("groups", None),
        P("groups", None),
    )
    return jax.shard_map(
        local, mesh=mesh, in_specs=placed, out_specs=P(("groups", "ctx"), "wide"), check_vma=False
    )
```

```python
import functools
import math

import jax
import jax.numpy as jnp
from jax import lax
from jax.experimental import pallas as pl
from jax.experimental.pallas import tpu as pltpu
from jax.sharding import PartitionSpec as P

D = 6144
QUERY_HEADS = 48
KEY_VALUE_HEADS = 8
HEAD_SIZE = 128


NEG_FILL = -1e30
EPSILON = 1e-05


def token_slots(expert_ids, slot_ids, capacity):
    in_window = jnp.logical_and(expert_ids == 0, slot_ids >= 0)
    picked = jnp.max(jnp.where(in_window, slot_ids, -1), axis=1)
    return jnp.where(picked >= 0, picked, capacity)


def other_experts(expert_ids, slot_of_token, capacity):
    partner = jnp.sum(expert_ids, axis=1)
    return jnp.zeros((capacity,), jnp.int32).at[slot_of_token].set(partner, mode="drop")


def expert_hidden(gate_sum, up_sum, square_sum, logit_sum, slot_other, model_width):
    inverse_rms = lax.rsqrt(square_sum / model_width + EPSILON)
    gate_value = gate_sum * inverse_rms[:, None]
    up_value = up_sum * inverse_rms[:, None]
    logit_value = logit_sum * inverse_rms[:, None]
    columns = jnp.arange(logit_value.shape[1], dtype=jnp.int32)
    partner_logit = jnp.sum(
        jnp.where(columns[None, :] == slot_other[:, None], logit_value, 0.0), axis=1
    )
    mixing = jax.nn.sigmoid(logit_value[:, 0] - partner_logit)
    return (jax.nn.silu(gate_value) * up_value * mixing[:, None]).astype(jnp.bfloat16)


def attention_kernel(offset_ref, q_ref, k_ref, v_ref, o_ref, *, per_shared, block_q, scale):
    seq = k_ref.shape[0]
    first = offset_ref[0] + pl.program_id(1) * block_q
    rows = first + lax.broadcasted_iota(jnp.int32, (block_q, seq), 0)
    cols = lax.broadcasted_iota(jnp.int32, (block_q, seq), 1)
    allowed = cols <= rows
    keys = k_ref[...]
    values = v_ref[...]
    for head in range(per_shared):
        query = q_ref[:, head * HEAD_SIZE : (head + 1) * HEAD_SIZE]
        scores = (
            lax.dot_general(
                query, keys, (((1,), (1,)), ((), ())), preferred_element_type=jnp.float32
            )
            * scale
        )
        masked = jnp.where(allowed, scores, NEG_FILL)
        row_max = jnp.max(masked, axis=1, keepdims=True)
        weights = jnp.exp(masked - row_max)
        total = jnp.sum(weights, axis=1, keepdims=True)
        acc = jnp.dot(weights.astype(jnp.bfloat16), values, preferred_element_type=jnp.float32)
        o_ref[:, head * HEAD_SIZE : (head + 1) * HEAD_SIZE] = (acc / total).astype(o_ref.dtype)


def attend(queries, packed_kv, offset, shared_heads, per_shared, interpret=False):
    rows_local = queries.shape[0]
    seq = packed_kv.shape[0]
    block_q = 128
    block_q = min(block_q, rows_local)
    width = per_shared * HEAD_SIZE
    kernel = functools.partial(
        attention_kernel,
        per_shared=per_shared,
        block_q=block_q,
        scale=1.0 / math.sqrt(HEAD_SIZE),
    )
    grid_spec = pltpu.PrefetchScalarGridSpec(
        num_scalar_prefetch=1,
        grid=(shared_heads, rows_local // block_q),
        in_specs=[
            pl.BlockSpec((block_q, width), lambda g, b, off: (b, g)),
            pl.BlockSpec((seq, HEAD_SIZE), lambda g, b, off: (0, g)),
            pl.BlockSpec((seq, HEAD_SIZE), lambda g, b, off: (0, shared_heads + g)),
        ],
        out_specs=pl.BlockSpec((block_q, width), lambda g, b, off: (b, g)),
    )
    return pl.pallas_call(
        kernel,
        grid_spec=grid_spec,
        out_shape=jax.ShapeDtypeStruct((rows_local, shared_heads * width), jnp.bfloat16),
        compiler_params=pltpu.CompilerParams(vmem_limit_bytes=48 * 1024 * 1024),
        interpret=interpret,
    )(offset, queries, packed_kv, packed_kv)


def pair_exchange(x, axis, count, bit):
    return lax.ppermute(x, axis, perm=[(i, i ^ bit) for i in range(count)])


def gather_rows(x, axis):
    count = lax.axis_size(axis)
    if count & (count - 1):
        return lax.all_gather(x, axis, axis=0, tiled=True)
    index = lax.axis_index(axis)
    out = x
    bit = 1
    while bit < count:
        other = pair_exchange(out, axis, count, bit)
        upper = (index // bit) % 2
        size = out.shape[0]
        both = jnp.zeros((2 * size,) + out.shape[1:], out.dtype)
        both = lax.dynamic_update_slice_in_dim(both, out, upper * size, 0)
        out = lax.dynamic_update_slice_in_dim(both, other, (1 - upper) * size, 0)
        bit *= 2
    return out


def gather_causal(x, axis):
    count = lax.axis_size(axis)
    if count != 4:
        return gather_rows(x, axis)
    index = lax.axis_index(axis)
    rows = x.shape[0]
    lower = lax.ppermute(x, axis, perm=[(0, 2), (1, 3)])
    pair = jnp.concatenate([x, lower], axis=0)
    other = pair_exchange(pair, axis, count, 1)
    partner = index ^ 1
    out = jnp.zeros((count * rows,) + x.shape[1:], x.dtype)
    for block, at in (
        (x, index),
        (lower, (index + 2) % 4),
        (other[:rows], partner),
        (other[rows:], (partner + 2) % 4),
    ):
        out = lax.dynamic_update_slice_in_dim(out, block, at * rows, 0)
    return out


def sum_rows(x, axis):
    count = lax.axis_size(axis)
    if count & (count - 1) or x.shape[0] % count:
        return lax.psum(x.astype(jnp.bfloat16), axis)
    index = lax.axis_index(axis)
    acc = x.astype(jnp.float32)
    bit = 1
    while bit < count // 2:
        half = acc.shape[0] // 2
        upper = (index // bit) % 2
        keep = lax.dynamic_slice_in_dim(acc, upper * half, half, 0)
        send = lax.dynamic_slice_in_dim(acc, (1 - upper) * half, half, 0)
        other = pair_exchange(send.astype(jnp.bfloat16), axis, count, bit)
        acc = keep + other.astype(jnp.float32)
        bit *= 2
    if bit < count:
        mine = acc.astype(jnp.bfloat16)
        other = pair_exchange(mine, axis, count, bit)
        upper = (index // bit) % 2
        low = jnp.where(upper == 0, mine, other).astype(jnp.float32)
        high = jnp.where(upper == 0, other, mine).astype(jnp.float32)
        acc = low + high
    out = acc.astype(jnp.bfloat16)
    bit = count // 4
    while bit >= 1:
        other = pair_exchange(out, axis, count, bit)
        upper = (index // bit) % 2
        size = out.shape[0]
        both = jnp.zeros((2 * size,) + out.shape[1:], out.dtype)
        both = lax.dynamic_update_slice_in_dim(both, out, upper * size, 0)
        out = lax.dynamic_update_slice_in_dim(both, other, (1 - upper) * size, 0)
        bit //= 2
    return out


def local(
    queries,
    key_rows,
    value_head_rows,
    residual,
    out_weight,
    norm_gain,
    router_weight,
    gate_weight,
    up_weight,
    down_weight,
    expert_ids,
    slot_ids,
):
    ctx_count = lax.axis_size("ctx")
    wide_index = lax.axis_index("wide")
    ctx_index = lax.axis_index("ctx")
    rows_local = queries.shape[0]
    heads_local = queries.shape[1] // HEAD_SIZE
    query_group_width = QUERY_HEADS // KEY_VALUE_HEADS
    shared_heads = max(1, heads_local // query_group_width)
    per_shared = heads_local // shared_heads
    first_shared = wide_index * heads_local // query_group_width
    key_used = lax.dynamic_slice_in_dim(
        key_rows, first_shared * HEAD_SIZE, shared_heads * HEAD_SIZE, 1
    )
    value_used = lax.dynamic_slice_in_dim(
        value_head_rows, first_shared * HEAD_SIZE, shared_heads * HEAD_SIZE, 1
    )
    packed_kv = gather_causal(jnp.concatenate([key_used, value_used], axis=1), "ctx")
    offset = jnp.reshape(ctx_index * rows_local, (1,)).astype(jnp.int32)
    attended = attend(queries, packed_kv, offset, shared_heads, per_shared)
    partial_out = jnp.dot(attended, out_weight, preferred_element_type=jnp.float32)
    head_sum = lax.psum_scatter(
        partial_out.astype(jnp.bfloat16), "wide", scatter_dimension=1, tiled=True
    ).astype(jnp.float32)
    resid = (residual.astype(jnp.float32) + head_sum).astype(jnp.bfloat16)
    seq_len = rows_local * ctx_count
    capacity = seq_len * 5 // 16
    width_local = resid.shape[1]
    wide_count = lax.axis_size("wide")
    chunk = capacity // wide_count
    slot_of_token = token_slots(expert_ids, slot_ids, capacity)
    partner = jnp.sum(expert_ids, axis=1)
    slot_local = lax.dynamic_slice_in_dim(slot_of_token, ctx_index * rows_local, rows_local)
    slot_ids_all = jnp.arange(capacity, dtype=jnp.int32)
    place = (slot_ids_all[:, None] == slot_local[None, :]).astype(jnp.bfloat16)
    own_rows = jnp.dot(place, resid, preferred_element_type=jnp.float32)
    buffer = sum_rows(own_rows, "ctx")
    buffer_wide = buffer.astype(jnp.float32)
    square_part = jnp.sum(buffer_wide * buffer_wide, axis=1)
    scaled = (buffer_wide * norm_gain.astype(jnp.float32)[None, :]).astype(jnp.bfloat16)
    both_part = jnp.dot(
        scaled,
        jnp.concatenate([gate_weight, up_weight], axis=1),
        preferred_element_type=jnp.float32,
    )
    logit_part = jnp.dot(scaled, router_weight, preferred_element_type=jnp.float32)
    hidden_local = gate_weight.shape[1]
    experts = logit_part.shape[1]
    pad = 128 - (experts + 1) % 128
    small = jnp.concatenate(
        [logit_part, square_part[:, None], jnp.zeros((capacity, pad), jnp.float32)], axis=1
    )
    both_sum = lax.psum_scatter(
        both_part.astype(jnp.bfloat16), "wide", scatter_dimension=0, tiled=True
    ).astype(jnp.float32)
    small_sum = lax.dynamic_slice_in_dim(
        sum_rows(small, "wide"), wide_index * chunk, chunk, 0
    ).astype(jnp.float32)
    gate_sum = both_sum[:, :hidden_local]
    up_sum = both_sum[:, hidden_local:]
    logit_sum = small_sum[:, :experts]
    square_sum = small_sum[:, experts]
    chunk_slots = wide_index * chunk + jnp.arange(chunk, dtype=jnp.int32)
    other_chunk = jnp.sum(
        jnp.where(chunk_slots[:, None] == slot_of_token[None, :], partner[None, :], 0), axis=1
    )
    hidden_chunk = expert_hidden(gate_sum, up_sum, square_sum, logit_sum, other_chunk, D)
    hidden = lax.all_gather(hidden_chunk, "wide", axis=0, tiled=True)
    expert_part = jnp.dot(hidden, down_weight, preferred_element_type=jnp.float32)
    expert_sum = sum_rows(expert_part, "ctx")
    pick = (slot_local[:, None] == slot_ids_all[None, :]).astype(jnp.bfloat16)
    moe_rows = jnp.dot(pick, expert_sum, preferred_element_type=jnp.float32)
    return (resid.astype(jnp.float32) + moe_rows).astype(jnp.bfloat16)


def solution(mesh):
    placed = (
        P(("groups", "ctx"), "wide"),
        P(("groups", "ctx"), None),
        P(("groups", "ctx"), None),
        P(("groups", "ctx"), "wide"),
        P("wide", None),
        P("wide"),
        P("wide", None),
        P("wide", "ctx"),
        P("wide", "ctx"),
        P("ctx", "wide"),
        P("groups", None),
        P("groups", None),
    )
    return jax.shard_map(
        local, mesh=mesh, in_specs=placed, out_specs=P(("groups", "ctx"), "wide"), check_vma=False
    )
```

```python
import functools
import math

import jax
import jax.numpy as jnp
from jax import lax
from jax.experimental import pallas as pl
from jax.experimental.pallas import tpu as pltpu
from jax.sharding import PartitionSpec as P

D = 6144
QUERY_HEADS = 48
KEY_VALUE_HEADS = 8
HEAD_SIZE = 128


NEG_FILL = -1e30
EPSILON = 1e-05


def token_slots(expert_ids, slot_ids, capacity):
    in_window = jnp.logical_and(expert_ids == 0, slot_ids >= 0)
    picked = jnp.max(jnp.where(in_window, slot_ids, -1), axis=1)
    return jnp.where(picked >= 0, picked, capacity)


def other_experts(expert_ids, slot_of_token, capacity):
    partner = jnp.sum(expert_ids, axis=1)
    return jnp.zeros((capacity,), jnp.int32).at[slot_of_token].set(partner, mode="drop")


def expert_hidden(gate_sum, up_sum, square_sum, logit_sum, slot_other, model_width):
    inverse_rms = lax.rsqrt(square_sum / model_width + EPSILON)
    gate_value = gate_sum * inverse_rms[:, None]
    up_value = up_sum * inverse_rms[:, None]
    logit_value = logit_sum * inverse_rms[:, None]
    columns = jnp.arange(logit_value.shape[1], dtype=jnp.int32)
    partner_logit = jnp.sum(
        jnp.where(columns[None, :] == slot_other[:, None], logit_value, 0.0), axis=1
    )
    mixing = jax.nn.sigmoid(logit_value[:, 0] - partner_logit)
    return (jax.nn.silu(gate_value) * up_value * mixing[:, None]).astype(jnp.bfloat16)


def attention_kernel(offset_ref, q_ref, k_ref, v_ref, o_ref, *, per_shared, block_q, scale):
    seq = k_ref.shape[0]
    first = offset_ref[0] + pl.program_id(1) * block_q
    rows = first + lax.broadcasted_iota(jnp.int32, (block_q, seq), 0)
    cols = lax.broadcasted_iota(jnp.int32, (block_q, seq), 1)
    allowed = cols <= rows
    keys = k_ref[...]
    values = v_ref[...]
    def one_head(head, carry):
        start = pl.multiple_of(head * HEAD_SIZE, HEAD_SIZE)
        query = q_ref[:, pl.ds(start, HEAD_SIZE)]
        scores = (
            lax.dot_general(
                query, keys, (((1,), (1,)), ((), ())), preferred_element_type=jnp.float32
            )
            * scale
        )
        masked = jnp.where(allowed, scores, NEG_FILL)
        row_max = jnp.max(masked, axis=1, keepdims=True)
        weights = jnp.exp(masked - row_max)
        total = jnp.sum(weights, axis=1, keepdims=True)
        acc = jnp.dot(weights.astype(jnp.bfloat16), values, preferred_element_type=jnp.float32)
        o_ref[:, pl.ds(start, HEAD_SIZE)] = (acc / total).astype(o_ref.dtype)
        return carry

    lax.fori_loop(0, per_shared, one_head, 0)


def attend(queries, packed_kv, offset, shared_heads, per_shared, interpret=False):
    rows_local = queries.shape[0]
    seq = packed_kv.shape[0]
    block_q = 256 if seq <= 2048 else 128
    block_q = min(block_q, rows_local)
    width = per_shared * HEAD_SIZE
    kernel = functools.partial(
        attention_kernel,
        per_shared=per_shared,
        block_q=block_q,
        scale=1.0 / math.sqrt(HEAD_SIZE),
    )
    grid_spec = pltpu.PrefetchScalarGridSpec(
        num_scalar_prefetch=1,
        grid=(shared_heads, rows_local // block_q),
        in_specs=[
            pl.BlockSpec((block_q, width), lambda g, b, off: (b, g)),
            pl.BlockSpec((seq, HEAD_SIZE), lambda g, b, off: (0, g)),
            pl.BlockSpec((seq, HEAD_SIZE), lambda g, b, off: (0, shared_heads + g)),
        ],
        out_specs=pl.BlockSpec((block_q, width), lambda g, b, off: (b, g)),
    )
    return pl.pallas_call(
        kernel,
        grid_spec=grid_spec,
        out_shape=jax.ShapeDtypeStruct((rows_local, shared_heads * width), jnp.bfloat16),
        compiler_params=pltpu.CompilerParams(vmem_limit_bytes=48 * 1024 * 1024),
        interpret=interpret,
    )(offset, queries, packed_kv, packed_kv)


def pair_exchange(x, axis, count, bit):
    return lax.ppermute(x, axis, perm=[(i, i ^ bit) for i in range(count)])


def gather_rows(x, axis):
    count = lax.axis_size(axis)
    if count & (count - 1):
        return lax.all_gather(x, axis, axis=0, tiled=True)
    index = lax.axis_index(axis)
    out = x
    bit = 1
    while bit < count:
        other = pair_exchange(out, axis, count, bit)
        upper = (index // bit) % 2
        size = out.shape[0]
        both = jnp.zeros((2 * size,) + out.shape[1:], out.dtype)
        both = lax.dynamic_update_slice_in_dim(both, out, upper * size, 0)
        out = lax.dynamic_update_slice_in_dim(both, other, (1 - upper) * size, 0)
        bit *= 2
    return out


def gather_causal(x, axis):
    count = lax.axis_size(axis)
    if count != 4:
        return gather_rows(x, axis)
    index = lax.axis_index(axis)
    rows = x.shape[0]
    lower = lax.ppermute(x, axis, perm=[(0, 2), (1, 3)])
    pair = jnp.concatenate([x, lower], axis=0)
    other = pair_exchange(pair, axis, count, 1)
    partner = index ^ 1
    out = jnp.zeros((count * rows,) + x.shape[1:], x.dtype)
    for block, at in (
        (x, index),
        (lower, (index + 2) % 4),
        (other[:rows], partner),
        (other[rows:], (partner + 2) % 4),
    ):
        out = lax.dynamic_update_slice_in_dim(out, block, at * rows, 0)
    return out


def sum_rows(x, axis):
    count = lax.axis_size(axis)
    if count & (count - 1) or x.shape[0] % count:
        return lax.psum(x.astype(jnp.bfloat16), axis)
    index = lax.axis_index(axis)
    acc = x.astype(jnp.float32)
    bit = 1
    while bit < count // 2:
        half = acc.shape[0] // 2
        upper = (index // bit) % 2
        keep = lax.dynamic_slice_in_dim(acc, upper * half, half, 0)
        send = lax.dynamic_slice_in_dim(acc, (1 - upper) * half, half, 0)
        other = pair_exchange(send.astype(jnp.bfloat16), axis, count, bit)
        acc = keep + other.astype(jnp.float32)
        bit *= 2
    if bit < count:
        mine = acc.astype(jnp.bfloat16)
        other = pair_exchange(mine, axis, count, bit)
        upper = (index // bit) % 2
        low = jnp.where(upper == 0, mine, other).astype(jnp.float32)
        high = jnp.where(upper == 0, other, mine).astype(jnp.float32)
        acc = low + high
    out = acc.astype(jnp.bfloat16)
    bit = count // 4
    while bit >= 1:
        other = pair_exchange(out, axis, count, bit)
        upper = (index // bit) % 2
        size = out.shape[0]
        both = jnp.zeros((2 * size,) + out.shape[1:], out.dtype)
        both = lax.dynamic_update_slice_in_dim(both, out, upper * size, 0)
        out = lax.dynamic_update_slice_in_dim(both, other, (1 - upper) * size, 0)
        bit //= 2
    return out


def local(
    queries,
    key_rows,
    value_head_rows,
    residual,
    out_weight,
    norm_gain,
    router_weight,
    gate_weight,
    up_weight,
    down_weight,
    expert_ids,
    slot_ids,
):
    ctx_count = lax.axis_size("ctx")
    wide_index = lax.axis_index("wide")
    ctx_index = lax.axis_index("ctx")
    rows_local = queries.shape[0]
    heads_local = queries.shape[1] // HEAD_SIZE
    query_group_width = QUERY_HEADS // KEY_VALUE_HEADS
    shared_heads = max(1, heads_local // query_group_width)
    per_shared = heads_local // shared_heads
    first_shared = wide_index * heads_local // query_group_width
    key_used = lax.dynamic_slice_in_dim(
        key_rows, first_shared * HEAD_SIZE, shared_heads * HEAD_SIZE, 1
    )
    value_used = lax.dynamic_slice_in_dim(
        value_head_rows, first_shared * HEAD_SIZE, shared_heads * HEAD_SIZE, 1
    )
    packed_kv = gather_causal(jnp.concatenate([key_used, value_used], axis=1), "ctx")
    offset = jnp.reshape(ctx_index * rows_local, (1,)).astype(jnp.int32)
    attended = attend(queries, packed_kv, offset, shared_heads, per_shared)
    partial_out = jnp.dot(attended, out_weight, preferred_element_type=jnp.float32)
    head_sum = lax.psum_scatter(
        partial_out.astype(jnp.bfloat16), "wide", scatter_dimension=1, tiled=True
    ).astype(jnp.float32)
    resid = (residual.astype(jnp.float32) + head_sum).astype(jnp.bfloat16)
    seq_len = rows_local * ctx_count
    capacity = seq_len * 5 // 16
    width_local = resid.shape[1]
    wide_count = lax.axis_size("wide")
    chunk = capacity // wide_count
    slot_of_token = token_slots(expert_ids, slot_ids, capacity)
    partner = jnp.sum(expert_ids, axis=1)
    slot_local = lax.dynamic_slice_in_dim(slot_of_token, ctx_index * rows_local, rows_local)
    slot_ids_all = jnp.arange(capacity, dtype=jnp.int32)
    place = (slot_ids_all[:, None] == slot_local[None, :]).astype(jnp.bfloat16)
    own_rows = jnp.dot(place, resid, preferred_element_type=jnp.float32)
    buffer = sum_rows(own_rows, "ctx")
    buffer_wide = buffer.astype(jnp.float32)
    square_part = jnp.sum(buffer_wide * buffer_wide, axis=1)
    scaled = (buffer_wide * norm_gain.astype(jnp.float32)[None, :]).astype(jnp.bfloat16)
    both_part = jnp.dot(
        scaled,
        jnp.concatenate([gate_weight, up_weight], axis=1),
        preferred_element_type=jnp.float32,
    )
    logit_part = jnp.dot(scaled, router_weight, preferred_element_type=jnp.float32)
    hidden_local = gate_weight.shape[1]
    experts = logit_part.shape[1]
    pad = 128 - (experts + 1) % 128
    small = jnp.concatenate(
        [logit_part, square_part[:, None], jnp.zeros((capacity, pad), jnp.float32)], axis=1
    )
    both_sum = lax.psum_scatter(
        both_part.astype(jnp.bfloat16), "wide", scatter_dimension=0, tiled=True
    ).astype(jnp.float32)
    small_sum = lax.dynamic_slice_in_dim(
        sum_rows(small, "wide"), wide_index * chunk, chunk, 0
    ).astype(jnp.float32)
    gate_sum = both_sum[:, :hidden_local]
    up_sum = both_sum[:, hidden_local:]
    logit_sum = small_sum[:, :experts]
    square_sum = small_sum[:, experts]
    chunk_slots = wide_index * chunk + jnp.arange(chunk, dtype=jnp.int32)
    other_chunk = jnp.sum(
        jnp.where(chunk_slots[:, None] == slot_of_token[None, :], partner[None, :], 0), axis=1
    )
    hidden_chunk = expert_hidden(gate_sum, up_sum, square_sum, logit_sum, other_chunk, D)
    hidden = lax.all_gather(hidden_chunk, "wide", axis=0, tiled=True)
    expert_part = jnp.dot(hidden, down_weight, preferred_element_type=jnp.float32)
    expert_sum = sum_rows(expert_part, "ctx")
    pick = (slot_local[:, None] == slot_ids_all[None, :]).astype(jnp.bfloat16)
    moe_rows = jnp.dot(pick, expert_sum, preferred_element_type=jnp.float32)
    return (resid.astype(jnp.float32) + moe_rows).astype(jnp.bfloat16)


def solution(mesh):
    placed = (
        P(("groups", "ctx"), "wide"),
        P(("groups", "ctx"), None),
        P(("groups", "ctx"), None),
        P(("groups", "ctx"), "wide"),
        P("wide", None),
        P("wide"),
        P("wide", None),
        P("wide", "ctx"),
        P("wide", "ctx"),
        P("ctx", "wide"),
        P("groups", None),
        P("groups", None),
    )
    return jax.shard_map(
        local, mesh=mesh, in_specs=placed, out_specs=P(("groups", "ctx"), "wide"), check_vma=False
    )
```
